128 devices in a mesh: section: 2 (over x_hi), expert: 16 (over z, y), tensor: 4 (over x_lo, core).
Axes of the slice: x: 4 (x_hi: 2, x_lo: 2; x = x_hi * 2 + x_lo), y: 4, z: 4, core: 2. Of those that a mesh axis runs over, the one named last changes fastest.
Arguments:
- tokens: bfloat16 [2, 1024, 3072], P(None, 'expert', 'tensor'), may hold values from -6 to 6
- norm_gain: float32 [2, 3072], P('section', 'tensor'), may hold values from 0.1 to 1.9
- expert_ids: int32 [2, 2, 1024, 2], P('section', None, 'expert'), may hold values from 0 to 7, all different within a row; in each aligned block of 64 rows (0 to 63, 64 to 127, ..., all dimensions but the last counted through in order) at most 24 rows name the same one
- gate_weights: float32 [2, 2, 1024, 2], P('section', None, 'expert'), may hold values from 0.1 to 0.9
- w_up: bfloat16 [2, 16, 3072, 4096], P('section', 'expert', None, 'tensor'), may hold values from -0.109375 to 0.109375
- w_down: bfloat16 [2, 16, 4096, 3072], P('section', 'expert', 'tensor'), may hold values from -0.0625 to 0.0625
Outputs:
- layer_states: bfloat16 [2, 2, 1024, 3072], P('section', None, 'expert', 'tensor')
The draws below stay inside these ranges and needn't reach their ends.
Inputs may be any that keep to these rules, and one draw needn't show every extreme that they name: `expert_ids`: the two ids of a token differ. In each layer and microbatch, among the 64 tokens of one index of expert, no expert is named by more than 24 of them, a bound that some block reaches.
All inputs are finite; a program needn't handle non-finite values.
Results may differ from the reference program's by a relative error of at most 0.0052.
Values may be sent and summed in bfloat16 or wider, within the bound.
No kernel may reach another device: no remote copies, remote signals or barrier semaphores. Data moves between devices by JAX's collectives and lax.ppermute only.
A program may use at most 64 MiB of HBM per device.

```python
import math
import jax
import jax.numpy as jnp
import numpy as np
from jax import lax

D = 3072
FFW = 8192
EXPERTS = 8
TOK_DEV = 64
MICRO = 2
COPIES = 2
SLOTS = 16
SLOT_FF = 4096
CAP = 24
TOKENS = 1024
LAYERS = 2
N_EXPERT = 16


def levels(rng, shape, shards, smallest, top_value):
    def one(position, parts):
        heights = jax.random.uniform(jax.random.fold_in(jax.random.fold_in(rng, 6), position), (parts,), jnp.float32, smallest / len(shards), top_value / len(shards))
        return jnp.repeat(jnp.exp(heights), shape[position] // parts).reshape((-1,) + (1,) * (len(shape) - position - 1))

    factor_of = one(*shards[0])
    for cut in shards[1:]:
        factor_of = factor_of * one(*cut)
    return factor_of


def assign_block(key, own, number, rows, count, top, bound, slope):
    sequence = jax.random.permutation(key, count)
    heavy_load, ordinary = shares(count, rows * top, bound, slope, True), shares(count, rows * top, bound, slope, False)
    places = jnp.arange(count)

    def named(lengths, offset_by):
        used = int((lengths > 0).sum())
        fixed = max(1, used // 4)
        moved = fixed + (places - fixed + offset_by * (used - fixed)) % max(1, count - fixed)
        return jnp.zeros((count,), jnp.int32).at[sequence[jnp.where(places < fixed, places, moved)]].set(jnp.asarray(lengths, jnp.int32))

    lengths = jnp.where(number % 4 == 0, named(heavy_load, number // 4), named(ordinary, number - number // 4 - 1))
    mixed = jax.random.permutation(jax.random.fold_in(own, 3), count)
    donor, taker = mixed[0:count // 2 * 2:2], mixed[1:count // 2 * 2:2]
    slack = jnp.minimum(lengths[donor] - 1, bound - lengths[taker]) // 2
    slack = jnp.where((donor == sequence[0]) | (taker == sequence[0]) | (lengths[taker] == 0), 0, jnp.maximum(slack, 0))
    moved = jax.random.randint(jax.random.fold_in(own, 4), (count // 2,), 0, 1 << 20) % (slack + 1)
    lengths = lengths.at[donor].add(-moved).at[taker].add(moved)
    labels = jnp.searchsorted(jnp.cumsum(lengths), jnp.arange(rows * top), side="right").astype(jnp.int32)
    table = labels.reshape(top, rows).T
    table = table[jax.random.permutation(jax.random.fold_in(own, 1), rows)]
    offset_by = jax.random.randint(jax.random.fold_in(own, 2), (rows, 1), 0, top)
    return jnp.take_along_axis(table, (jnp.arange(top)[None, :] + offset_by) % top, axis=1)


def shares(number_of, total, bound, skew, full):
    weights = [(1 << 20) // math.isqrt(grade ** skew) + 1 for grade in range(1, number_of + 1)]
    largest = bound if full else min(bound, max(-(-total // number_of), total * weights[0] // sum(weights)))
    least = 1 if total - largest >= number_of - 1 else 0
    holding, surplus = [largest] + [least] * (number_of - 1), total - largest - least * (number_of - 1)
    while surplus > 0:
        free = [i for i in range(1, number_of) if holding[i] < largest] or [i for i in range(1, number_of) if holding[i] < bound]
        mass, remaining = sum([weights[i] for i in free]), surplus
        for i in free:
            addition = min(bound - holding[i], max(1, remaining * weights[i] // mass), surplus)
            holding[i] = holding[i] + addition
            surplus = surplus - addition
    return np.array(holding)


def centred(rng, extent, scale, reach, pieces=(), kind=jnp.bfloat16):
    result = jax.random.normal(rng, extent, jnp.float32) * scale
    if len(pieces) > 0:
        result = levels(rng, extent, pieces, -0.22, 0.18) * result
    return jnp.clip(result, min=-reach, max=reach).astype(kind)


def setup_inputs(seed: int = 0) -> dict:
    streams_of = jax.random.split(jax.random.key(seed), 7)
    tokens = centred(streams_of[0], (MICRO, TOKENS, D), 1.0, 6.0, ((1, 16), (2, 4)))
    norm_gain = jnp.clip(1.0 + 0.18 * jax.random.normal(streams_of[1], (LAYERS, D), jnp.float32), 0.1, 1.9)
    expert_ids_keys = jax.random.split(jax.random.fold_in(streams_of[2], 1), LAYERS * MICRO * TOKENS // TOK_DEV)
    expert_ids_turns = jax.random.permutation(jax.random.fold_in(streams_of[2], 3), LAYERS * MICRO * TOKENS // TOK_DEV)
    expert_ids = jax.vmap(lambda own, number: assign_block(jax.random.fold_in(streams_of[2], 2), own, number, TOK_DEV, EXPERTS, 2, CAP, 2))(expert_ids_keys, expert_ids_turns).reshape((LAYERS, MICRO, TOKENS, 2))
    gate_weights = jnp.clip(0.1 + 0.79999997 * jax.random.uniform(streams_of[3], (LAYERS, MICRO, TOKENS, 2), jnp.float32) ** levels(streams_of[3], (LAYERS, MICRO, TOKENS, 2), ((0, 2), (2, 16)), -0.2, 0.2), 0.1, 0.9)
    w_up = centred(streams_of[4], (LAYERS, SLOTS, D, SLOT_FF), D ** -0.5, 0.109375, ((0, 2), (1, 16), (3, 4)))
    w_down = centred(streams_of[5], (LAYERS, SLOTS, SLOT_FF, D), FFW ** -0.5, 0.0625, ((0, 2), (1, 16), (2, 4)))
    return {"tokens": tokens, "norm_gain": norm_gain, "expert_ids": expert_ids, "gate_weights": gate_weights, "w_up": w_up, "w_down": w_down}


def expert_ffn(rows, up_proj, down_proj):
    summed_up = jnp.dot(rows, up_proj, preferred_element_type=jnp.float32)
    hidden = jax.nn.silu(summed_up).astype(jnp.bfloat16)
    return jnp.dot(hidden, down_proj, preferred_element_type=jnp.float32).astype(jnp.bfloat16)

def reference(tokens, norm_gain, expert_ids, gate_weights, w_up, w_down):
    limit = N_EXPERT * CAP
    states = []
    for layer in range(LAYERS):
        states.append([])
    for micro in range(MICRO):
        x = tokens[micro]
        for layer in range(LAYERS):
            up_full = w_up[layer].reshape(EXPERTS, COPIES, D, SLOT_FF).transpose(0, 2, 1, 3).reshape(EXPERTS, D, FFW)
            down_full = w_down[layer].reshape(EXPERTS, FFW, D)
            xf = x.astype(jnp.float32)
            sums = lax.optimization_barrier(jnp.sum(xf * xf, axis=1))
            normed = (xf * lax.rsqrt(sums / D + 1e-05)[:, None] * norm_gain[layer][None, :]).astype(jnp.bfloat16)
            flat = expert_ids[layer, micro].reshape(-1).astype(jnp.int32)
            onehot = (flat[:, None] == jnp.arange(EXPERTS, dtype=jnp.int32)[None, :]).astype(jnp.int32)
            slot = lax.optimization_barrier(jnp.sum((jnp.cumsum(onehot, axis=0) - onehot) * onehot, axis=1)).astype(jnp.int32)
            dest = (flat * limit + slot).astype(jnp.int32)
            source = jnp.full((EXPERTS * limit,), -1, jnp.int32).at[dest].set((jnp.arange(2 * TOKENS, dtype=jnp.int32) // 2).astype(jnp.int32))
            filled = source >= 0
            rows = jnp.where(filled[:, None], jnp.take(normed, jnp.maximum(source, 0), axis=0), jnp.zeros((), jnp.bfloat16))
            rows = rows.astype(jnp.bfloat16).reshape(EXPERTS, limit, D)
            outs = lax.map(lambda a: expert_ffn(a[0], a[1], a[2]), (rows, up_full, down_full))
            picked = jnp.take(outs.reshape(-1, D), dest, axis=0).astype(jnp.float32).reshape(TOKENS, 2, D)
            mixed = xf + lax.optimization_barrier(jnp.sum(picked * gate_weights[layer, micro][:, :, None], axis=1))
            x = mixed.astype(jnp.bfloat16)
            states[layer].append(x)
    return jnp.stack([jnp.stack(s, axis=0) for s in states], axis=0)
```

```python
import jax
import jax.numpy as jnp
from jax import lax
from jax.sharding import PartitionSpec as P

D = 3072
EXPERTS = 8


def from_behind(block, axis, distance):
    devices = range(lax.axis_size(axis))
    route = [(i - distance, i) for i in devices if i - distance in devices]
    return lax.ppermute(block, axis, route)


def swap(block, axis, bit):
    n = lax.axis_size(axis)
    return lax.ppermute(block, axis, [(i, i ^ bit) for i in range(n)])


def shards(tokens, norm_gain, expert_ids, gate_weights, w_up, w_down):
    segments = lax.axis_size("section")
    n_exp = lax.axis_size("expert")
    segment_pos = lax.axis_index("section")
    t_pos = lax.axis_index("tensor")
    x_lo = t_pos // 2
    core = t_pos % 2
    micro = tokens.shape[0]
    rows_here = tokens.shape[1]
    quarter = tokens.shape[2]
    capacity = max(3 * rows_here // 8, 2 * rows_here // EXPERTS)
    gain_full = lax.all_gather(norm_gain[0], "tensor", axis=0, tiled=True)
    up_local = w_up[0]
    down_local = w_down[0]
    local_count = up_local.shape[0]
    copies = n_exp * local_count // EXPERTS
    collected = jnp.zeros((micro, rows_here, quarter), jnp.bfloat16)
    carried = jnp.zeros((rows_here, quarter), jnp.bfloat16)
    total_steps = micro + segments - 1
    x_first = x_lo == 0
    core_first = core == 0
    for step in range(total_steps):
        which = step - segment_pos
        which_safe = jnp.clip(which, 0, micro - 1)
        entering = tokens[min(step, micro - 1)]
        current = jnp.where(segment_pos == 0, entering, carried)
        routes = lax.dynamic_index_in_dim(expert_ids[0], which_safe, 0, keepdims=False)
        weights = lax.dynamic_index_in_dim(gate_weights[0], which_safe, 0, keepdims=False)
        xf = current.astype(jnp.float32)
        other = swap(current, "tensor", 2)
        half_rows = jnp.where(
            x_first,
            jnp.concatenate([current, other], axis=1),
            jnp.concatenate([other, current], axis=1),
        )
        flat = routes.reshape(-1)
        onehot = (flat[:, None] == jnp.arange(EXPERTS, dtype=jnp.int32)[None, :]).astype(jnp.int32)
        slot = jnp.sum((jnp.cumsum(onehot, axis=0) - onehot) * onehot, axis=1)
        dest = flat * capacity + slot
        source = (
            jnp.full((EXPERTS * capacity,), -1, jnp.int32)
            .at[dest]
            .set(jnp.arange(2 * rows_here, dtype=jnp.int32) // 2)
        )
        filled = source >= 0
        outgoing = jnp.where(
            filled[:, None],
            jnp.take(half_rows, jnp.maximum(source, 0), axis=0),
            jnp.zeros((), jnp.bfloat16),
        )
        outgoing = outgoing.reshape(EXPERTS, capacity, 2 * quarter)
        outgoing = jnp.repeat(outgoing, copies, axis=0).reshape(
            n_exp, local_count, capacity, 2 * quarter
        )
        mine = lax.all_to_all(outgoing, "expert", split_axis=0, concat_axis=0, tiled=True)
        theirs = swap(mine, "tensor", 1)
        lo_q = lambda a: a[..., :quarter]
        hi_q = lambda a: a[..., quarter:]
        first = jnp.where(core_first, mine, theirs)
        second = jnp.where(core_first, theirs, mine)
        rows = jnp.concatenate([lo_q(first), lo_q(second), hi_q(first), hi_q(second)], axis=-1)
        rf = rows.astype(jnp.float32)
        sums = jnp.sum(rf * rf, axis=-1)
        normed = (rf * lax.rsqrt(sums / D + 1e-05)[..., None] * gain_full).astype(jnp.bfloat16)
        summed_up = jnp.einsum(
            "sekd,edf->sekf", normed, up_local, preferred_element_type=jnp.float32
        )
        hidden = jax.nn.silu(summed_up).astype(jnp.bfloat16)
        partial_out = jnp.einsum(
            "sekf,efd->sekd", hidden, down_local, preferred_element_type=jnp.float32
        )
        pq = [partial_out[..., q * quarter:(q + 1) * quarter] for q in range(4)]
        keep = jnp.where(
            core_first,
            jnp.concatenate([pq[0], pq[2]], axis=-1),
            jnp.concatenate([pq[1], pq[3]], axis=-1),
        )
        give = jnp.where(
            core_first,
            jnp.concatenate([pq[1], pq[3]], axis=-1),
            jnp.concatenate([pq[0], pq[2]], axis=-1),
        )
        got = swap(give.astype(jnp.bfloat16), "tensor", 1)
        chip_sum = (keep + got.astype(jnp.float32)).astype(jnp.bfloat16)
        returned = lax.all_to_all(chip_sum, "expert", split_axis=0, concat_axis=0, tiled=True)
        summed = jnp.sum(
            returned.reshape(EXPERTS, copies, capacity, 2 * quarter).astype(jnp.float32), axis=1
        )
        picked = jnp.take(summed.reshape(-1, 2 * quarter), dest, axis=0)
        picked = picked.reshape(rows_here, 2, 2 * quarter)
        y_half = jnp.sum(picked * weights[:, :, None], axis=1)
        y_keep = jnp.where(x_first, y_half[:, :quarter], y_half[:, quarter:])
        y_give = jnp.where(x_first, y_half[:, quarter:], y_half[:, :quarter])
        y_got = swap(y_give, "tensor", 2)
        mixed = xf + (y_keep + y_got)
        produced = mixed.astype(jnp.bfloat16)
        chosen = (jnp.arange(micro, dtype=jnp.int32) == which)[:, None, None]
        collected = jnp.where(chosen, produced[None], collected)
        if step + 1 < total_steps:
            carried = from_behind(produced, "section", 1)
    return collected[None]


def solution(mesh):
    placed = (
        P(None, "expert", "tensor"),
        P("section", "tensor"),
        P("section", None, "expert", None),
        P("section", None, "expert", None),
        P("section", "expert", None, "tensor"),
        P("section", "expert", "tensor", None),
    )
    return jax.shard_map(
        shards,
        mesh=mesh,
        in_specs=placed,
        out_specs=P("section", None, "expert", "tensor"),
        check_vma=False,
    )
```

```python
import jax
import jax.numpy as jnp
from jax import lax
from jax.sharding import PartitionSpec as P

D = 3072
EXPERTS = 8


def from_behind(block, axis, distance):
    devices = range(lax.axis_size(axis))
    route = [(i - distance, i) for i in devices if i - distance in devices]
    return lax.ppermute(block, axis, route)


def swap(block, axis, bit):
    n = lax.axis_size(axis)
    return lax.ppermute(block, axis, [(i, i ^ bit) for i in range(n)])


def shards(tokens, norm_gain, expert_ids, gate_weights, w_up, w_down):
    segments = lax.axis_size("section")
    n_exp = lax.axis_size("expert")
    segment_pos = lax.axis_index("section")
    t_pos = lax.axis_index("tensor")
    x_lo = t_pos // 2
    core = t_pos % 2
    micro = tokens.shape[0]
    rows_here = tokens.shape[1]
    quarter = tokens.shape[2]
    capacity = max(3 * rows_here // 8, 2 * rows_here // EXPERTS)
    gain = norm_gain[0]
    gain_from = [gain, swap(gain, "tensor", 1), swap(gain, "tensor", 2), swap(gain, "tensor", 3)]
    gain_full = jnp.concatenate(
        [
            jnp.where(t_pos == q, gain_from[0],
                      jnp.where(t_pos ^ 1 == q, gain_from[1],
                                jnp.where(t_pos ^ 2 == q, gain_from[2], gain_from[3])))
            for q in range(4)
        ]
    )
    up_local = w_up[0]
    down_local = w_down[0]
    local_count = up_local.shape[0]
    copies = n_exp * local_count // EXPERTS
    collected = jnp.zeros((micro, rows_here, quarter), jnp.bfloat16)
    carried = jnp.zeros((rows_here, 2 * quarter), jnp.bfloat16)
    total_steps = micro + segments - 1
    x_first = x_lo == 0
    core_first = core == 0
    tokens_other = swap(tokens, "tensor", 2)
    tokens_half = jnp.where(
        x_first,
        jnp.concatenate([tokens, tokens_other], axis=2),
        jnp.concatenate([tokens_other, tokens], axis=2),
    )
    for step in range(total_steps):
        which = step - segment_pos
        which_safe = jnp.clip(which, 0, micro - 1)
        entering = tokens_half[min(step, micro - 1)]
        half_rows = jnp.where(segment_pos == 0, entering, carried)
        routes = lax.dynamic_index_in_dim(expert_ids[0], which_safe, 0, keepdims=False)
        weights = lax.dynamic_index_in_dim(gate_weights[0], which_safe, 0, keepdims=False)
        flat = routes.reshape(-1)
        onehot = (flat[:, None] == jnp.arange(EXPERTS, dtype=jnp.int32)[None, :]).astype(jnp.int32)
        slot = jnp.sum((jnp.cumsum(onehot, axis=0) - onehot) * onehot, axis=1)
        dest = flat * capacity + slot
        source = (
            jnp.full((EXPERTS * capacity,), -1, jnp.int32)
            .at[dest]
            .set(jnp.arange(2 * rows_here, dtype=jnp.int32) // 2)
        )
        filled = source >= 0
        outgoing = jnp.where(
            filled[:, None],
            jnp.take(half_rows, jnp.maximum(source, 0), axis=0),
            jnp.zeros((), jnp.bfloat16),
        )
        outgoing = outgoing.reshape(EXPERTS, capacity, 2 * quarter)
        outgoing = jnp.repeat(outgoing, copies, axis=0).reshape(
            n_exp, local_count, capacity, 2 * quarter
        )
        mine = lax.all_to_all(outgoing, "expert", split_axis=0, concat_axis=0, tiled=True)
        theirs = swap(mine, "tensor", 1)
        lo_q = lambda a: a[..., :quarter]
        hi_q = lambda a: a[..., quarter:]
        first = jnp.where(core_first, mine, theirs)
        second = jnp.where(core_first, theirs, mine)
        rows = jnp.concatenate([lo_q(first), lo_q(second), hi_q(first), hi_q(second)], axis=-1)
        rf = rows.astype(jnp.float32)
        sums = jnp.sum(rf * rf, axis=-1)
        normed = (rf * lax.rsqrt(sums / D + 1e-05)[..., None] * gain_full).astype(jnp.bfloat16)
        summed_up = jnp.einsum(
            "sekd,edf->sekf", normed, up_local, preferred_element_type=jnp.float32
        )
        hidden = jax.nn.silu(summed_up).astype(jnp.bfloat16)
        partial_out = jnp.einsum(
            "sekf,efd->sekd", hidden, down_local, preferred_element_type=jnp.float32
        )
        pq = [partial_out[..., q * quarter:(q + 1) * quarter] for q in range(4)]
        keep = jnp.where(
            core_first,
            jnp.concatenate([pq[0], pq[2]], axis=-1),
            jnp.concatenate([pq[1], pq[3]], axis=-1),
        )
        give = jnp.where(
            core_first,
            jnp.concatenate([pq[1], pq[3]], axis=-1),
            jnp.concatenate([pq[0], pq[2]], axis=-1),
        )
        got = swap(give.astype(jnp.bfloat16), "tensor", 1)
        chip_sum = (keep + got.astype(jnp.float32)).astype(jnp.bfloat16)
        returned = lax.all_to_all(chip_sum, "expert", split_axis=0, concat_axis=0, tiled=True)
        summed = jnp.sum(
            returned.reshape(EXPERTS, copies, capacity, 2 * quarter).astype(jnp.float32), axis=1
        )
        picked = jnp.take(summed.reshape(-1, 2 * quarter), dest, axis=0)
        picked = picked.reshape(rows_here, 2, 2 * quarter)
        y_half = jnp.sum(picked * weights[:, :, None], axis=1)
        y_got = swap(y_half, "tensor", 2)
        produced_half = (half_rows.astype(jnp.float32) + (y_half + y_got)).astype(jnp.bfloat16)
        produced = jnp.where(x_first, produced_half[:, :quarter], produced_half[:, quarter:])
        chosen = (jnp.arange(micro, dtype=jnp.int32) == which)[:, None, None]
        collected = jnp.where(chosen, produced[None], collected)
        if step + 1 < total_steps:
            carried = from_behind(produced_half, "section", 1)
    return collected[None]


def solution(mesh):
    placed = (
        P(None, "expert", "tensor"),
        P("section", "tensor"),
        P("section", None, "expert", None),
        P("section", None, "expert", None),
        P("section", "expert", None, "tensor"),
        P("section", "expert", "tensor", None),
    )
    return jax.shard_map(
        shards,
        mesh=mesh,
        in_specs=placed,
        out_specs=P("section", None, "expert", "tensor"),
        check_vma=False,
    )
```

```python
import jax
import jax.numpy as jnp
from jax import lax
from jax.sharding import PartitionSpec as P

D = 3072
EXPERTS = 8


def from_behind(block, axis, distance):
    devices = range(lax.axis_size(axis))
    route = [(i - distance, i) for i in devices if i - distance in devices]
    return lax.ppermute(block, axis, route)


def swap(block, axis, bit):
    n = lax.axis_size(axis)
    return lax.ppermute(block, axis, [(i, i ^ bit) for i in range(n)])


def shards(tokens, norm_gain, expert_ids, gate_weights, w_up, w_down):
    segments = lax.axis_size("section")
    n_exp = lax.axis_size("expert")
    segment_pos = lax.axis_index("section")
    t_pos = lax.axis_index("tensor")
    x_lo = t_pos // 2
    core = t_pos % 2
    micro = tokens.shape[0]
    rows_here = tokens.shape[1]
    quarter = tokens.shape[2]
    capacity = max(3 * rows_here // 8, 2 * rows_here // EXPERTS)
    gain = norm_gain[0]
    gain_from = [gain, swap(gain, "tensor", 1), swap(gain, "tensor", 2), swap(gain, "tensor", 3)]
    gain_full = jnp.concatenate(
        [
            jnp.where(t_pos == q, gain_from[0],
                      jnp.where(t_pos ^ 1 == q, gain_from[1],
                                jnp.where(t_pos ^ 2 == q, gain_from[2], gain_from[3])))
            for q in range(4)
        ]
    )
    up_local = w_up[0]
    down_local = w_down[0]
    local_count = up_local.shape[0]
    copies = n_exp * local_count // EXPERTS
    collected = jnp.zeros((micro, rows_here, quarter), jnp.bfloat16)
    total_steps = micro + segments - 1
    x_first = x_lo == 0
    core_first = core == 0

    def to_half(own, other):
        return jnp.where(
            x_first,
            jnp.concatenate([own, other], axis=-1),
            jnp.concatenate([other, own], axis=-1),
        )

    tokens_half = to_half(tokens, swap(tokens, "tensor", 2))
    routes_all = expert_ids[0].reshape(micro, -1)
    onehot_all = (routes_all[..., None] == jnp.arange(EXPERTS, dtype=jnp.int32)).astype(jnp.int32)
    slot_all = jnp.sum((jnp.cumsum(onehot_all, axis=1) - onehot_all) * onehot_all, axis=2)
    dest_all = routes_all * capacity + slot_all
    source_all = (
        jnp.full((micro, EXPERTS * capacity), -1, jnp.int32)
        .at[jnp.arange(micro)[:, None], dest_all]
        .set(jnp.broadcast_to(jnp.arange(2 * rows_here, dtype=jnp.int32) // 2, dest_all.shape))
    )
    n_t = lax.axis_size("tensor")
    cross_route = [
        (s * n_t + t, (s + 1) * n_t + (t ^ 2)) for s in range(segments - 1) for t in range(n_t)
    ]
    carried = jnp.zeros((rows_here, 2 * quarter), jnp.bfloat16)
    for step in range(total_steps):
        which = step - segment_pos
        which_safe = jnp.clip(which, 0, micro - 1)
        entering = tokens_half[min(step, micro - 1)]
        half_rows = jnp.where(segment_pos == 0, entering, carried)
        weights = lax.dynamic_index_in_dim(gate_weights[0], which_safe, 0, keepdims=False)
        dest = lax.dynamic_index_in_dim(dest_all, which_safe, 0, keepdims=False)
        source = lax.dynamic_index_in_dim(source_all, which_safe, 0, keepdims=False)
        filled = source >= 0
        outgoing = jnp.where(
            filled[:, None],
            jnp.take(half_rows, jnp.maximum(source, 0), axis=0),
            jnp.zeros((), jnp.bfloat16),
        )
        outgoing = outgoing.reshape(EXPERTS, capacity, 2 * quarter)
        outgoing = jnp.repeat(outgoing, copies, axis=0).reshape(
            n_exp, local_count, capacity, 2 * quarter
        )
        mine = lax.all_to_all(outgoing, "expert", split_axis=0, concat_axis=0, tiled=True)
        theirs = swap(mine, "tensor", 1)
        lo_q = lambda a: a[..., :quarter]
        hi_q = lambda a: a[..., quarter:]
        first = jnp.where(core_first, mine, theirs)
        second = jnp.where(core_first, theirs, mine)
        rows = jnp.concatenate([lo_q(first), lo_q(second), hi_q(first), hi_q(second)], axis=-1)
        rf = rows.astype(jnp.float32)
        sums = jnp.sum(rf * rf, axis=-1)
        normed = (rf * lax.rsqrt(sums / D + 1e-05)[..., None] * gain_full).astype(jnp.bfloat16)
        summed_up = jnp.einsum(
            "sekd,edf->sekf", normed, up_local, preferred_element_type=jnp.float32
        )
        hidden = jax.nn.silu(summed_up).astype(jnp.bfloat16)
        partial_out = jnp.einsum(
            "sekf,efd->sekd", hidden, down_local, preferred_element_type=jnp.float32
        )
        pq = [partial_out[..., q * quarter:(q + 1) * quarter] for q in range(4)]
        keep = jnp.where(
            core_first,
            jnp.concatenate([pq[0], pq[2]], axis=-1),
            jnp.concatenate([pq[1], pq[3]], axis=-1),
        )
        give = jnp.where(
            core_first,
            jnp.concatenate([pq[1], pq[3]], axis=-1),
            jnp.concatenate([pq[0], pq[2]], axis=-1),
        )
        got = swap(give.astype(jnp.bfloat16), "tensor", 1)
        chip_sum = (keep + got.astype(jnp.float32)).astype(jnp.bfloat16)
        returned = lax.all_to_all(chip_sum, "expert", split_axis=0, concat_axis=0, tiled=True)
        summed = jnp.sum(
            returned.reshape(EXPERTS, copies, capacity, 2 * quarter).astype(jnp.float32), axis=1
        )
        picked = jnp.take(summed.reshape(-1, 2 * quarter), dest, axis=0)
        picked = picked.reshape(rows_here, 2, 2 * quarter)
        y_half = jnp.sum(picked * weights[:, :, None], axis=1)
        y_keep = jnp.where(x_first, y_half[:, :quarter], y_half[:, quarter:])
        y_give = jnp.where(x_first, y_half[:, quarter:], y_half[:, :quarter])
        y_got = swap(y_give, "tensor", 2)
        xf = jnp.where(x_first, half_rows[:, :quarter], half_rows[:, quarter:]).astype(jnp.float32)
        mixed = xf + (y_keep + y_got)
        produced = mixed.astype(jnp.bfloat16)
        chosen = (jnp.arange(micro, dtype=jnp.int32) == which)[:, None, None]
        collected = jnp.where(chosen, produced[None], collected)
        if step + 1 < total_steps:
            carried = to_half(
                from_behind(produced, "section", 1),
                lax.ppermute(produced, ("section", "tensor"), cross_route),
            )
    return collected[None]


def solution(mesh):
    placed = (
        P(None, "expert", "tensor"),
        P("section", "tensor"),
        P("section", None, "expert", None),
        P("section", None, "expert", None),
        P("section", "expert", None, "tensor"),
        P("section", "expert", "tensor", None),
    )
    return jax.shard_map(
        shards,
        mesh=mesh,
        in_specs=placed,
        out_specs=P("section", None, "expert", "tensor"),
        check_vma=False,
    )
```

```python
import jax
import jax.numpy as jnp
from jax import lax
from jax.sharding import PartitionSpec as P

D = 3072
EXPERTS = 8


def from_behind(block, axis, distance):
    devices = range(lax.axis_size(axis))
    route = [(i - distance, i) for i in devices if i - distance in devices]
    return lax.ppermute(block, axis, route)


def swap(block, axis, bit):
    n = lax.axis_size(axis)
    return lax.ppermute(block, axis, [(i, i ^ bit) for i in range(n)])


def shards(tokens, norm_gain, expert_ids, gate_weights, w_up, w_down):
    segments = lax.axis_size("section")
    n_exp = lax.axis_size("expert")
    segment_pos = lax.axis_index("section")
    t_pos = lax.axis_index("tensor")
    x_lo = t_pos // 2
    core = t_pos % 2
    micro = tokens.shape[0]
    rows_here = tokens.shape[1]
    quarter = tokens.shape[2]
    capacity = max(3 * rows_here // 8, 2 * rows_here // EXPERTS)
    gain = norm_gain[0]
    gain_from = [gain, swap(gain, "tensor", 1), swap(gain, "tensor", 2), swap(gain, "tensor", 3)]
    gain_full = jnp.concatenate(
        [
            jnp.where(t_pos == q, gain_from[0],
                      jnp.where(t_pos ^ 1 == q, gain_from[1],
                                jnp.where(t_pos ^ 2 == q, gain_from[2], gain_from[3])))
            for q in range(4)
        ]
    )
    up_local = w_up[0]
    down_local = w_down[0]
    local_count = up_local.shape[0]
    copies = n_exp * local_count // EXPERTS
    collected = jnp.zeros((micro, rows_here, quarter), jnp.bfloat16)
    total_steps = micro + segments - 1
    x_first = x_lo == 0
    core_first = core == 0

    def to_half(own, other):
        return jnp.where(
            x_first,
            jnp.concatenate([own, other], axis=-1),
            jnp.concatenate([other, own], axis=-1),
        )

    tokens_half = to_half(tokens, swap(tokens, "tensor", 2))
    routes_all = expert_ids[0].reshape(micro, -1)
    onehot_all = (routes_all[..., None] == jnp.arange(EXPERTS, dtype=jnp.int32)).astype(jnp.int32)
    slot_all = jnp.sum((jnp.cumsum(onehot_all, axis=1) - onehot_all) * onehot_all, axis=2)
    dest_all = routes_all * capacity + slot_all
    source_all = jnp.stack(
        [
            jnp.full((EXPERTS * capacity,), -1, jnp.int32)
            .at[dest_all[m]]
            .set(jnp.arange(2 * rows_here, dtype=jnp.int32) // 2)
            for m in range(micro)
        ]
    )
    n_t = lax.axis_size("tensor")
    cross_route = [
        (s * n_t + t, (s + 1) * n_t + (t ^ 2)) for s in range(segments - 1) for t in range(n_t)
    ]
    carried = jnp.zeros((rows_here, 2 * quarter), jnp.bfloat16)
    for step in range(total_steps):
        which = step - segment_pos
        which_safe = jnp.clip(which, 0, micro - 1)
        entering = tokens_half[min(step, micro - 1)]
        half_rows = jnp.where(segment_pos == 0, entering, carried)
        weights = lax.dynamic_index_in_dim(gate_weights[0], which_safe, 0, keepdims=False)
        dest = lax.dynamic_index_in_dim(dest_all, which_safe, 0, keepdims=False)
        source = lax.dynamic_index_in_dim(source_all, which_safe, 0, keepdims=False)
        filled = source >= 0
        outgoing = jnp.where(
            filled[:, None],
            jnp.take(half_rows, jnp.maximum(source, 0), axis=0),
            jnp.zeros((), jnp.bfloat16),
        )
        outgoing = outgoing.reshape(EXPERTS, capacity, 2 * quarter)
        outgoing = jnp.repeat(outgoing, copies, axis=0).reshape(
            n_exp, local_count, capacity, 2 * quarter
        )
        mine = lax.all_to_all(outgoing, "expert", split_axis=0, concat_axis=0, tiled=True)
        theirs = swap(mine, "tensor", 1)
        lo_q = lambda a: a[..., :quarter]
        hi_q = lambda a: a[..., quarter:]
        first = jnp.where(core_first, mine, theirs)
        second = jnp.where(core_first, theirs, mine)
        rows = jnp.concatenate([lo_q(first), lo_q(second), hi_q(first), hi_q(second)], axis=-1)
        rf = rows.astype(jnp.float32)
        sums = jnp.sum(rf * rf, axis=-1)
        normed = (rf * lax.rsqrt(sums / D + 1e-05)[..., None] * gain_full).astype(jnp.bfloat16)
        summed_up = jnp.einsum(
            "sekd,edf->sekf", normed, up_local, preferred_element_type=jnp.float32
        )
        hidden = jax.nn.silu(summed_up).astype(jnp.bfloat16)
        partial_out = jnp.einsum(
            "sekf,efd->sekd", hidden, down_local, preferred_element_type=jnp.float32
        )
        pq = [partial_out[..., q * quarter:(q + 1) * quarter] for q in range(4)]
        keep = jnp.where(
            core_first,
            jnp.concatenate([pq[0], pq[2]], axis=-1),
            jnp.concatenate([pq[1], pq[3]], axis=-1),
        )
        give = jnp.where(
            core_first,
            jnp.concatenate([pq[1], pq[3]], axis=-1),
            jnp.concatenate([pq[0], pq[2]], axis=-1),
        )
        got = swap(give.astype(jnp.bfloat16), "tensor", 1)
        chip_sum = (keep + got.astype(jnp.float32)).astype(jnp.bfloat16)
        returned = lax.all_to_all(chip_sum, "expert", split_axis=0, concat_axis=0, tiled=True)
        summed = jnp.sum(
            returned.reshape(EXPERTS, copies, capacity, 2 * quarter).astype(jnp.float32), axis=1
        )
        picked = jnp.take(summed.reshape(-1, 2 * quarter), dest, axis=0)
        picked = picked.reshape(rows_here, 2, 2 * quarter)
        y_half = jnp.sum(picked * weights[:, :, None], axis=1)
        y_keep = jnp.where(x_first, y_half[:, :quarter], y_half[:, quarter:])
        y_give = jnp.where(x_first, y_half[:, quarter:], y_half[:, :quarter])
        y_got = swap(y_give, "tensor", 2)
        xf = jnp.where(x_first, half_rows[:, :quarter], half_rows[:, quarter:]).astype(jnp.float32)
        mixed = xf + (y_keep + y_got)
        produced = mixed.astype(jnp.bfloat16)
        chosen = (jnp.arange(micro, dtype=jnp.int32) == which)[:, None, None]
        collected = jnp.where(chosen, produced[None], collected)
        if step + 1 < total_steps:
            carried = to_half(
                from_behind(produced, "section", 1),
                lax.ppermute(produced, ("section", "tensor"), cross_route),
            )
    return collected[None]


def solution(mesh):
    placed = (
        P(None, "expert", "tensor"),
        P("section", "tensor"),
        P("section", None, "expert", None),
        P("section", None, "expert", None),
        P("section", "expert", None, "tensor"),
        P("section", "expert", "tensor", None),
    )
    return jax.shard_map(
        shards,
        mesh=mesh,
        in_specs=placed,
        out_specs=P("section", None, "expert", "tensor"),
        check_vma=False,
    )
```

```python
import jax
import jax.numpy as jnp
from jax import lax
from jax.sharding import PartitionSpec as P

D = 3072
EXPERTS = 8


def from_behind(block, axis, distance):
    devices = range(lax.axis_size(axis))
    route = [(i - distance, i) for i in devices if i - distance in devices]
    return lax.ppermute(block, axis, route)


def swap(block, axis, bit):
    n = lax.axis_size(axis)
    return lax.ppermute(block, axis, [(i, i ^ bit) for i in range(n)])


def shards(tokens, norm_gain, expert_ids, gate_weights, w_up, w_down):
    segments = lax.axis_size("section")
    n_exp = lax.axis_size("expert")
    segment_pos = lax.axis_index("section")
    t_pos = lax.axis_index("tensor")
    x_lo = t_pos // 2
    core = t_pos % 2
    micro = tokens.shape[0]
    rows_here = tokens.shape[1]
    quarter = tokens.shape[2]
    capacity = max(3 * rows_here // 8, 2 * rows_here // EXPERTS)
    gain = norm_gain[0]
    gain_from = [gain, swap(gain, "tensor", 1), swap(gain, "tensor", 2), swap(gain, "tensor", 3)]
    gain_full = jnp.concatenate(
        [
            jnp.where(t_pos == q, gain_from[0],
                      jnp.where(t_pos ^ 1 == q, gain_from[1],
                                jnp.where(t_pos ^ 2 == q, gain_from[2], gain_from[3])))
            for q in range(4)
        ]
    )
    up_local = w_up[0]
    down_local = w_down[0]
    local_count = up_local.shape[0]
    copies = n_exp * local_count // EXPERTS
    collected = jnp.zeros((micro, rows_here, quarter), jnp.bfloat16)
    total_steps = micro + segments - 1
    x_first = x_lo == 0
    core_first = core == 0

    def to_half(own, other):
        return jnp.where(
            x_first,
            jnp.concatenate([own, other], axis=-1),
            jnp.concatenate([other, own], axis=-1),
        )

    tokens_half = to_half(tokens, swap(tokens, "tensor", 2))
    routes_all = expert_ids[0].reshape(micro, -1)
    onehot_all = (routes_all[..., None] == jnp.arange(EXPERTS, dtype=jnp.int32)).astype(jnp.int32)
    slot_all = jnp.sum((jnp.cumsum(onehot_all, axis=1) - onehot_all) * onehot_all, axis=2)
    dest_all = routes_all * capacity + slot_all
    source_all = jnp.stack(
        [
            jnp.full((EXPERTS * capacity,), -1, jnp.int32)
            .at[dest_all[m]]
            .set(jnp.arange(2 * rows_here, dtype=jnp.int32) // 2)
            for m in range(micro)
        ]
    )
    n_t = lax.axis_size("tensor")
    cross_route = [
        (s * n_t + t, (s + 1) * n_t + (t ^ 2)) for s in range(segments - 1) for t in range(n_t)
    ]
    def layer_step(step, carried, collected):
        which = step - segment_pos
        which_safe = jnp.clip(which, 0, micro - 1)
        entering = lax.dynamic_index_in_dim(
            tokens_half, jnp.minimum(step, micro - 1), 0, keepdims=False
        )
        half_rows = jnp.where(segment_pos == 0, entering, carried)
        weights = lax.dynamic_index_in_dim(gate_weights[0], which_safe, 0, keepdims=False)
        dest = lax.dynamic_index_in_dim(dest_all, which_safe, 0, keepdims=False)
        source = lax.dynamic_index_in_dim(source_all, which_safe, 0, keepdims=False)
        filled = source >= 0
        outgoing = jnp.where(
            filled[:, None],
            jnp.take(half_rows, jnp.maximum(source, 0), axis=0),
            jnp.zeros((), jnp.bfloat16),
        )
        outgoing = outgoing.reshape(EXPERTS, capacity, 2 * quarter)
        outgoing = jnp.repeat(outgoing, copies, axis=0).reshape(
            n_exp, local_count, capacity, 2 * quarter
        )
        mine = lax.all_to_all(outgoing, "expert", split_axis=0, concat_axis=0, tiled=True)
        theirs = swap(mine, "tensor", 1)
        lo_q = lambda a: a[..., :quarter]
        hi_q = lambda a: a[..., quarter:]
        first = jnp.where(core_first, mine, theirs)
        second = jnp.where(core_first, theirs, mine)
        rows = jnp.concatenate([lo_q(first), lo_q(second), hi_q(first), hi_q(second)], axis=-1)
        rf = rows.astype(jnp.float32)
        sums = jnp.sum(rf * rf, axis=-1)
        normed = (rf * lax.rsqrt(sums / D + 1e-05)[..., None] * gain_full).astype(jnp.bfloat16)
        summed_up = jnp.einsum(
            "sekd,edf->sekf", normed, up_local, preferred_element_type=jnp.float32
        )
        hidden = jax.nn.silu(summed_up).astype(jnp.bfloat16)
        partial_out = jnp.einsum(
            "sekf,efd->sekd", hidden, down_local, preferred_element_type=jnp.float32
        )
        pq = [partial_out[..., q * quarter:(q + 1) * quarter] for q in range(4)]
        keep = jnp.where(
            core_first,
            jnp.concatenate([pq[0], pq[2]], axis=-1),
            jnp.concatenate([pq[1], pq[3]], axis=-1),
        )
        give = jnp.where(
            core_first,
            jnp.concatenate([pq[1], pq[3]], axis=-1),
            jnp.concatenate([pq[0], pq[2]], axis=-1),
        )
        got = swap(give.astype(jnp.bfloat16), "tensor", 1)
        chip_sum = (keep + got.astype(jnp.float32)).astype(jnp.bfloat16)
        returned = lax.all_to_all(chip_sum, "expert", split_axis=0, concat_axis=0, tiled=True)
        summed = jnp.sum(
            returned.reshape(EXPERTS, copies, capacity, 2 * quarter).astype(jnp.float32), axis=1
        )
        picked = jnp.take(summed.reshape(-1, 2 * quarter), dest, axis=0)
        picked = picked.reshape(rows_here, 2, 2 * quarter)
        y_half = jnp.sum(picked * weights[:, :, None], axis=1)
        y_keep = jnp.where(x_first, y_half[:, :quarter], y_half[:, quarter:])
        y_give = jnp.where(x_first, y_half[:, quarter:], y_half[:, :quarter])
        y_got = swap(y_give, "tensor", 2)
        xf = jnp.where(x_first, half_rows[:, :quarter], half_rows[:, quarter:]).astype(jnp.float32)
        mixed = xf + (y_keep + y_got)
        produced = mixed.astype(jnp.bfloat16)
        chosen = (jnp.arange(micro, dtype=jnp.int32) == which)[:, None, None]
        collected = jnp.where(chosen, produced[None], collected)
        return produced, collected

    def looped(step, state):
        carried, collected = state
        produced, collected = layer_step(step, carried, collected)
        carried = to_half(
            from_behind(produced, "section", 1),
            lax.ppermute(produced, ("section", "tensor"), cross_route),
        )
        return carried, collected

    carried = jnp.zeros((rows_here, 2 * quarter), jnp.bfloat16)
    carried, collected = lax.fori_loop(0, total_steps - 1, looped, (carried, collected))
    _, collected = layer_step(total_steps - 1, carried, collected)
    return collected[None]


def solution(mesh):
    placed = (
        P(None, "expert", "tensor"),
        P("section", "tensor"),
        P("section", None, "expert", None),
        P("section", None, "expert", None),
        P("section", "expert", None, "tensor"),
        P("section", "expert", "tensor", None),
    )
    return jax.shard_map(
        shards,
        mesh=mesh,
        in_specs=placed,
        out_specs=P("section", None, "expert", "tensor"),
        check_vma=False,
    )
```

```python
import jax
import jax.numpy as jnp
from jax import lax
from jax.sharding import PartitionSpec as P

D = 3072
EXPERTS = 8


def from_behind(block, axis, distance):
    devices = range(lax.axis_size(axis))
    route = [(i - distance, i) for i in devices if i - distance in devices]
    return lax.ppermute(block, axis, route)


def swap(block, axis, bit):
    n = lax.axis_size(axis)
    return lax.ppermute(block, axis, [(i, i ^ bit) for i in range(n)])


def shards(tokens, norm_gain, expert_ids, gate_weights, w_up, w_down):
    segments = lax.axis_size("section")
    n_exp = lax.axis_size("expert")
    segment_pos = lax.axis_index("section")
    t_pos = lax.axis_index("tensor")
    x_lo = t_pos // 2
    core = t_pos % 2
    micro = tokens.shape[0]
    rows_here = tokens.shape[1]
    quarter = tokens.shape[2]
    capacity = max(3 * rows_here // 8, 2 * rows_here // EXPERTS)
    gain = norm_gain[0]
    gain_from = [gain, swap(gain, "tensor", 1), swap(gain, "tensor", 2), swap(gain, "tensor", 3)]
    gain_full = jnp.concatenate(
        [
            jnp.where(t_pos == q, gain_from[0],
                      jnp.where(t_pos ^ 1 == q, gain_from[1],
                                jnp.where(t_pos ^ 2 == q, gain_from[2], gain_from[3])))
            for q in range(4)
        ]
    )
    up_local = w_up[0]
    down_local = w_down[0]
    local_count = up_local.shape[0]
    copies = n_exp * local_count // EXPERTS
    collected = jnp.zeros((micro, rows_here, quarter), jnp.bfloat16)
    total_steps = micro + segments - 1
    x_first = x_lo == 0
    core_first = core == 0

    def to_half(own, other):
        return jnp.where(
            x_first,
            jnp.concatenate([own, other], axis=-1),
            jnp.concatenate([other, own], axis=-1),
        )

    tokens_half = to_half(tokens, swap(tokens, "tensor", 2))
    routes_all = expert_ids[0].reshape(micro, -1)
    onehot_all = (routes_all[..., None] == jnp.arange(EXPERTS, dtype=jnp.int32)).astype(jnp.int32)
    slot_all = jnp.sum((jnp.cumsum(onehot_all, axis=1) - onehot_all) * onehot_all, axis=2)
    dest_all = routes_all * capacity + slot_all
    source_all = jnp.stack(
        [
            jnp.full((EXPERTS * capacity,), -1, jnp.int32)
            .at[dest_all[m]]
            .set(jnp.arange(2 * rows_here, dtype=jnp.int32) // 2)
            for m in range(micro)
        ]
    )
    n_t = lax.axis_size("tensor")
    cross_route = [
        (s * n_t + t, (s + 1) * n_t + (t ^ 2)) for s in range(segments - 1) for t in range(n_t)
    ]
    def layer_step(step, carried, collected):
        which = step - segment_pos
        which_safe = jnp.clip(which, 0, micro - 1)
        entering = lax.dynamic_index_in_dim(
            tokens_half, jnp.minimum(step, micro - 1), 0, keepdims=False
        )
        half_rows = jnp.where(segment_pos == 0, entering, carried)
        weights = lax.dynamic_index_in_dim(gate_weights[0], which_safe, 0, keepdims=False)
        dest = lax.dynamic_index_in_dim(dest_all, which_safe, 0, keepdims=False)
        source = lax.dynamic_index_in_dim(source_all, which_safe, 0, keepdims=False)
        filled = source >= 0
        outgoing = jnp.where(
            filled[:, None],
            jnp.take(half_rows, jnp.maximum(source, 0), axis=0),
            jnp.zeros((), jnp.bfloat16),
        )
        outgoing = outgoing.reshape(EXPERTS, capacity, 2 * quarter)
        outgoing = jnp.repeat(outgoing, copies, axis=0).reshape(
            n_exp, local_count, capacity, 2 * quarter
        )
        mine = lax.all_to_all(outgoing, "expert", split_axis=0, concat_axis=0, tiled=True)
        theirs = swap(mine, "tensor", 1)
        lo_q = lambda a: a[..., :quarter]
        hi_q = lambda a: a[..., quarter:]
        first = jnp.where(core_first, mine, theirs)
        second = jnp.where(core_first, theirs, mine)
        rows = jnp.concatenate([lo_q(first), lo_q(second), hi_q(first), hi_q(second)], axis=-1)
        rf = rows.astype(jnp.float32)
        sums = jnp.sum(rf * rf, axis=-1)
        normed = (rf * lax.rsqrt(sums / D + 1e-05)[..., None] * gain_full).astype(jnp.bfloat16)
        summed_up = jnp.einsum(
            "sekd,edf->sekf", normed, up_local, preferred_element_type=jnp.float32
        )
        hidden = jax.nn.silu(summed_up).astype(jnp.bfloat16)
        partial_out = jnp.einsum(
            "sekf,efd->sekd", hidden, down_local, preferred_element_type=jnp.float32
        ).astype(jnp.bfloat16)
        pq = [partial_out[..., q * quarter:(q + 1) * quarter] for q in range(4)]
        keep = jnp.where(
            core_first,
            jnp.concatenate([pq[0], pq[2]], axis=-1),
            jnp.concatenate([pq[1], pq[3]], axis=-1),
        )
        give = jnp.where(
            core_first,
            jnp.concatenate([pq[1], pq[3]], axis=-1),
            jnp.concatenate([pq[0], pq[2]], axis=-1),
        )
        got = swap(give, "tensor", 1)
        chip_sum = (keep.astype(jnp.float32) + got.astype(jnp.float32)).astype(jnp.bfloat16)
        returned = lax.all_to_all(chip_sum, "expert", split_axis=0, concat_axis=0, tiled=True)
        summed = jnp.sum(
            returned.reshape(EXPERTS, copies, capacity, 2 * quarter).astype(jnp.float32), axis=1
        )
        picked = jnp.take(summed.reshape(-1, 2 * quarter), dest, axis=0)
        picked = picked.reshape(rows_here, 2, 2 * quarter)
        y_half = jnp.sum(picked * weights[:, :, None], axis=1)
        y_keep = jnp.where(x_first, y_half[:, :quarter], y_half[:, quarter:])
        y_give = jnp.where(x_first, y_half[:, quarter:], y_half[:, :quarter])
        y_got = swap(y_give.astype(jnp.bfloat16), "tensor", 2).astype(jnp.float32)
        xf = jnp.where(x_first, half_rows[:, :quarter], half_rows[:, quarter:]).astype(jnp.float32)
        mixed = xf + (y_keep + y_got)
        produced = mixed.astype(jnp.bfloat16)
        chosen = (jnp.arange(micro, dtype=jnp.int32) == which)[:, None, None]
        collected = jnp.where(chosen, produced[None], collected)
        return produced, collected

    def looped(step, state):
        carried, collected = state
        produced, collected = layer_step(step, carried, collected)
        carried = to_half(
            from_behind(produced, "section", 1),
            lax.ppermute(produced, ("section", "tensor"), cross_route),
        )
        return carried, collected

    carried = jnp.zeros((rows_here, 2 * quarter), jnp.bfloat16)
    carried, collected = lax.fori_loop(0, total_steps - 1, looped, (carried, collected))
    _, collected = layer_step(total_steps - 1, carried, collected)
    return collected[None]


def solution(mesh):
    placed = (
        P(None, "expert", "tensor"),
        P("section", "tensor"),
        P("section", None, "expert", None),
        P("section", None, "expert", None),
        P("section", "expert", None, "tensor"),
        P("section", "expert", "tensor", None),
    )
    return jax.shard_map(
        shards,
        mesh=mesh,
        in_specs=placed,
        out_specs=P("section", None, "expert", "tensor"),
        check_vma=False,
    )
```

```python
import jax
import jax.numpy as jnp
from jax import lax
from jax.sharding import PartitionSpec as P

D = 3072
EXPERTS = 8


def from_behind(block, axis, distance):
    devices = range(lax.axis_size(axis))
    route = [(i - distance, i) for i in devices if i - distance in devices]
    return lax.ppermute(block, axis, route)


def swap(block, axis, bit):
    n = lax.axis_size(axis)
    return lax.ppermute(block, axis, [(i, i ^ bit) for i in range(n)])


def shards(tokens, norm_gain, expert_ids, gate_weights, w_up, w_down):
    segments = lax.axis_size("section")
    n_exp = lax.axis_size("expert")
    segment_pos = lax.axis_index("section")
    t_pos = lax.axis_index("tensor")
    x_lo = t_pos // 2
    core = t_pos % 2
    micro = tokens.shape[0]
    rows_here = tokens.shape[1]
    quarter = tokens.shape[2]
    capacity = max(3 * rows_here // 8, 2 * rows_here // EXPERTS)
    gain = norm_gain[0]
    gain_from = [gain, swap(gain, "tensor", 1), swap(gain, "tensor", 2), swap(gain, "tensor", 3)]
    gain_full = jnp.concatenate(
        [
            jnp.where(t_pos == q, gain_from[0],
                      jnp.where(t_pos ^ 1 == q, gain_from[1],
                                jnp.where(t_pos ^ 2 == q, gain_from[2], gain_from[3])))
            for q in range(4)
        ]
    )
    up_local = w_up[0]
    down_local = w_down[0]
    local_count = up_local.shape[0]
    copies = n_exp * local_count // EXPERTS
    collected = jnp.zeros((micro, rows_here, quarter), jnp.bfloat16)
    total_steps = micro + segments - 1
    x_first = x_lo == 0
    core_first = core == 0

    def to_half(own, other):
        return jnp.where(
            x_first,
            jnp.concatenate([own, other], axis=-1),
            jnp.concatenate([other, own], axis=-1),
        )

    tokens_half = to_half(tokens, swap(tokens, "tensor", 2))
    routes_all = expert_ids[0].reshape(micro, -1)
    onehot_all = (routes_all[..., None] == jnp.arange(EXPERTS, dtype=jnp.int32)).astype(jnp.int32)
    slot_all = jnp.sum((jnp.cumsum(onehot_all, axis=1) - onehot_all) * onehot_all, axis=2)
    dest_all = routes_all * capacity + slot_all
    source_all = jnp.stack(
        [
            jnp.full((EXPERTS * capacity,), -1, jnp.int32)
            .at[dest_all[m]]
            .set(jnp.arange(2 * rows_here, dtype=jnp.int32) // 2)
            for m in range(micro)
        ]
    )
    n_t = lax.axis_size("tensor")
    cross_route = [
        (s * n_t + t, (s + 1) * n_t + (t ^ 2)) for s in range(segments - 1) for t in range(n_t)
    ]
    first_section = segment_pos == 0

    def a2a(block):
        return lax.all_to_all(block, "expert", split_axis=0, concat_axis=0, tiled=True)

    def dispatch(half_rows, m):
        source = source_all[m]
        filled = source >= 0
        outgoing = jnp.where(
            filled[:, None],
            jnp.take(half_rows, jnp.maximum(source, 0), axis=0),
            jnp.zeros((), jnp.bfloat16),
        )
        outgoing = outgoing.reshape(EXPERTS, capacity, 2 * quarter)
        return jnp.repeat(outgoing, copies, axis=0).reshape(
            n_exp, local_count, capacity, 2 * quarter
        )

    def expert(mine):
        theirs = swap(mine, "tensor", 1)
        lo_q = lambda a: a[..., :quarter]
        hi_q = lambda a: a[..., quarter:]
        first = jnp.where(core_first, mine, theirs)
        second = jnp.where(core_first, theirs, mine)
        rows = jnp.concatenate([lo_q(first), lo_q(second), hi_q(first), hi_q(second)], axis=-1)
        rf = rows.astype(jnp.float32)
        sums = jnp.sum(rf * rf, axis=-1)
        normed = (rf * lax.rsqrt(sums / D + 1e-05)[..., None] * gain_full).astype(jnp.bfloat16)
        summed_up = jnp.einsum(
            "sekd,edf->sekf", normed, up_local, preferred_element_type=jnp.float32
        )
        hidden = jax.nn.silu(summed_up).astype(jnp.bfloat16)
        partial_out = jnp.einsum(
            "sekf,efd->sekd", hidden, down_local, preferred_element_type=jnp.float32
        ).astype(jnp.bfloat16)
        pq = [partial_out[..., q * quarter:(q + 1) * quarter] for q in range(4)]
        keep = jnp.where(
            core_first,
            jnp.concatenate([pq[0], pq[2]], axis=-1),
            jnp.concatenate([pq[1], pq[3]], axis=-1),
        )
        give = jnp.where(
            core_first,
            jnp.concatenate([pq[1], pq[3]], axis=-1),
            jnp.concatenate([pq[0], pq[2]], axis=-1),
        )
        got = swap(give, "tensor", 1)
        return (keep.astype(jnp.float32) + got.astype(jnp.float32)).astype(jnp.bfloat16)

    def combine(returned, m, half_rows):
        summed = jnp.sum(
            returned.reshape(EXPERTS, copies, capacity, 2 * quarter).astype(jnp.float32), axis=1
        )
        picked = jnp.take(summed.reshape(-1, 2 * quarter), dest_all[m], axis=0)
        picked = picked.reshape(rows_here, 2, 2 * quarter)
        y_half = jnp.sum(picked * gate_weights[0, m][:, :, None], axis=1)
        y_keep = jnp.where(x_first, y_half[:, :quarter], y_half[:, quarter:])
        y_give = jnp.where(x_first, y_half[:, quarter:], y_half[:, :quarter])
        y_got = swap(y_give.astype(jnp.bfloat16), "tensor", 2).astype(jnp.float32)
        xf = jnp.where(x_first, half_rows[:, :quarter], half_rows[:, quarter:]).astype(jnp.float32)
        return (xf + (y_keep + y_got)).astype(jnp.bfloat16)

    def send(produced):
        return to_half(
            from_behind(produced, "section", 1),
            lax.ppermute(produced, ("section", "tensor"), cross_route),
        )

    rows_0 = tokens_half[0]
    rows_1 = tokens_half[1]
    partial_a = expert(a2a(dispatch(rows_0, 0)))
    merged = lax.all_to_all(
        jnp.stack([partial_a, dispatch(rows_1, 1)], axis=1), "expert", split_axis=0, concat_axis=0, tiled=True
    )
    back_a, recv_b = merged[:, 0], merged[:, 1]
    out_00 = combine(back_a, 0, rows_0)
    next_0 = send(out_00)
    partial_b = expert(recv_b)
    shared = a2a(jnp.where(first_section, partial_b, dispatch(next_0, 0)))
    out_01 = combine(shared, 1, rows_1)
    next_1 = send(out_01)
    partial_c = expert(shared)
    merged = lax.all_to_all(
        jnp.stack([partial_c, dispatch(next_1, 1)], axis=1), "expert", split_axis=0, concat_axis=0, tiled=True
    )
    back_c, recv_d = merged[:, 0], merged[:, 1]
    out_10 = combine(back_c, 0, next_0)
    partial_d = expert(recv_d)
    out_11 = combine(a2a(partial_d), 1, next_1)
    collected = jnp.stack(
        [jnp.where(first_section, out_00, out_10), jnp.where(first_section, out_01, out_11)]
    )
    return collected[None]


def solution(mesh):
    placed = (
        P(None, "expert", "tensor"),
        P("section", "tensor"),
        P("section", None, "expert", None),
        P("section", None, "expert", None),
        P("section", "expert", None, "tensor"),
        P("section", "expert", "tensor", None),
    )
    return jax.shard_map(
        shards,
        mesh=mesh,
        in_specs=placed,
        out_specs=P("section", None, "expert", "tensor"),
        check_vma=False,
    )
```

```python
import jax
import jax.numpy as jnp
from jax import lax
from jax.sharding import PartitionSpec as P

D = 3072
EXPERTS = 8


def from_behind(block, axis, distance):
    devices = range(lax.axis_size(axis))
    route = [(i - distance, i) for i in devices if i - distance in devices]
    return lax.ppermute(block, axis, route)


def swap(block, axis, bit):
    n = lax.axis_size(axis)
    return lax.ppermute(block, axis, [(i, i ^ bit) for i in range(n)])


def shards(tokens, norm_gain, expert_ids, gate_weights, w_up, w_down):
    segments = lax.axis_size("section")
    n_exp = lax.axis_size("expert")
    segment_pos = lax.axis_index("section")
    t_pos = lax.axis_index("tensor")
    x_lo = t_pos // 2
    core = t_pos % 2
    micro = tokens.shape[0]
    rows_here = tokens.shape[1]
    quarter = tokens.shape[2]
    capacity = max(3 * rows_here // 8, 2 * rows_here // EXPERTS)
    gain = norm_gain[0]
    gain_from = [gain, swap(gain, "tensor", 1), swap(gain, "tensor", 2), swap(gain, "tensor", 3)]
    gain_full = jnp.concatenate(
        [
            jnp.where(t_pos == q, gain_from[0],
                      jnp.where(t_pos ^ 1 == q, gain_from[1],
                                jnp.where(t_pos ^ 2 == q, gain_from[2], gain_from[3])))
            for q in range(4)
        ]
    )
    up_local = w_up[0]
    down_local = w_down[0]
    local_count = up_local.shape[0]
    copies = n_exp * local_count // EXPERTS
    collected = jnp.zeros((micro, rows_here, quarter), jnp.bfloat16)
    total_steps = micro + segments - 1
    x_first = x_lo == 0
    core_first = core == 0

    def to_half(own, other):
        return jnp.where(
            x_first,
            jnp.concatenate([own, other], axis=-1),
            jnp.concatenate([other, own], axis=-1),
        )

    tokens_half = to_half(tokens, swap(tokens, "tensor", 2))
    routes_all = expert_ids[0].reshape(micro, -1)
    onehot_all = (routes_all[..., None] == jnp.arange(EXPERTS, dtype=jnp.int32)).astype(jnp.int32)
    slot_all = jnp.sum((jnp.cumsum(onehot_all, axis=1) - onehot_all) * onehot_all, axis=2)
    dest_all = routes_all * capacity + slot_all
    source_all = jnp.stack(
        [
            jnp.full((EXPERTS * capacity,), -1, jnp.int32)
            .at[dest_all[m]]
            .set(jnp.arange(2 * rows_here, dtype=jnp.int32) // 2)
            for m in range(micro)
        ]
    )
    n_t = lax.axis_size("tensor")
    cross_route = [
        (s * n_t + t, (s + 1) * n_t + (t ^ 2)) for s in range(segments - 1) for t in range(n_t)
    ]
    down_q = [down_local[..., q * quarter:(q + 1) * quarter] for q in range(4)]
    down_even = jnp.concatenate([down_q[0], down_q[2]], axis=-1)
    down_odd = jnp.concatenate([down_q[1], down_q[3]], axis=-1)
    down_keep = jnp.where(core_first, down_even, down_odd)
    down_give = jnp.where(core_first, down_odd, down_even)

    def layer_step(step, carried, collected):
        which = step - segment_pos
        which_safe = jnp.clip(which, 0, micro - 1)
        entering = lax.dynamic_index_in_dim(
            tokens_half, jnp.minimum(step, micro - 1), 0, keepdims=False
        )
        half_rows = jnp.where(segment_pos == 0, entering, carried)
        weights = lax.dynamic_index_in_dim(gate_weights[0], which_safe, 0, keepdims=False)
        dest = lax.dynamic_index_in_dim(dest_all, which_safe, 0, keepdims=False)
        source = lax.dynamic_index_in_dim(source_all, which_safe, 0, keepdims=False)
        filled = source >= 0
        outgoing = jnp.where(
            filled[:, None],
            jnp.take(half_rows, jnp.maximum(source, 0), axis=0),
            jnp.zeros((), jnp.bfloat16),
        )
        outgoing = outgoing.reshape(EXPERTS, capacity, 2 * quarter)
        outgoing = jnp.repeat(outgoing, copies, axis=0).reshape(
            n_exp, local_count, capacity, 2 * quarter
        )
        mine = lax.all_to_all(outgoing, "expert", split_axis=0, concat_axis=0, tiled=True)
        theirs = swap(mine, "tensor", 1)
        lo_q = lambda a: a[..., :quarter]
        hi_q = lambda a: a[..., quarter:]
        first = jnp.where(core_first, mine, theirs)
        second = jnp.where(core_first, theirs, mine)
        rows = jnp.concatenate([lo_q(first), lo_q(second), hi_q(first), hi_q(second)], axis=-1)
        rf = rows.astype(jnp.float32)
        sums = jnp.sum(rf * rf, axis=-1)
        normed = (rf * lax.rsqrt(sums / D + 1e-05)[..., None] * gain_full).astype(jnp.bfloat16)
        summed_up = jnp.einsum(
            "sekd,edf->sekf", normed, up_local, preferred_element_type=jnp.float32
        )
        hidden = jax.nn.silu(summed_up).astype(jnp.bfloat16)
        give = jnp.einsum(
            "sekf,efd->sekd", hidden, down_give, preferred_element_type=jnp.float32
        ).astype(jnp.bfloat16)
        got = swap(give, "tensor", 1)
        keep = jnp.einsum(
            "sekf,efd->sekd", hidden, down_keep, preferred_element_type=jnp.float32
        )
        chip_sum = (keep + got.astype(jnp.float32)).astype(jnp.bfloat16)
        returned = lax.all_to_all(chip_sum, "expert", split_axis=0, concat_axis=0, tiled=True)
        summed = jnp.sum(
            returned.reshape(EXPERTS, copies, capacity, 2 * quarter).astype(jnp.float32), axis=1
        )
        picked = jnp.take(summed.reshape(-1, 2 * quarter), dest, axis=0)
        picked = picked.reshape(rows_here, 2, 2 * quarter)
        y_half = jnp.sum(picked * weights[:, :, None], axis=1)
        y_keep = jnp.where(x_first, y_half[:, :quarter], y_half[:, quarter:])
        y_give = jnp.where(x_first, y_half[:, quarter:], y_half[:, :quarter])
        y_got = swap(y_give.astype(jnp.bfloat16), "tensor", 2).astype(jnp.float32)
        xf = jnp.where(x_first, half_rows[:, :quarter], half_rows[:, quarter:]).astype(jnp.float32)
        mixed = xf + (y_keep + y_got)
        produced = mixed.astype(jnp.bfloat16)
        chosen = (jnp.arange(micro, dtype=jnp.int32) == which)[:, None, None]
        collected = jnp.where(chosen, produced[None], collected)
        return produced, collected

    def looped(step, state):
        carried, collected = state
        produced, collected = layer_step(step, carried, collected)
        carried = to_half(
            from_behind(produced, "section", 1),
            lax.ppermute(produced, ("section", "tensor"), cross_route),
        )
        return carried, collected

    carried = jnp.zeros((rows_here, 2 * quarter), jnp.bfloat16)
    carried, collected = lax.fori_loop(0, total_steps - 1, looped, (carried, collected))
    _, collected = layer_step(total_steps - 1, carried, collected)
    return collected[None]


def solution(mesh):
    placed = (
        P(None, "expert", "tensor"),
        P("section", "tensor"),
        P("section", None, "expert", None),
        P("section", None, "expert", None),
        P("section", "expert", None, "tensor"),
        P("section", "expert", "tensor", None),
    )
    return jax.shard_map(
        shards,
        mesh=mesh,
        in_specs=placed,
        out_specs=P("section", None, "expert", "tensor"),
        check_vma=False,
    )
```

```python
import jax
import jax.numpy as jnp
from jax import lax
from jax.sharding import PartitionSpec as P

D = 3072
EXPERTS = 8


def from_behind(block, axis, distance):
    devices = range(lax.axis_size(axis))
    route = [(i - distance, i) for i in devices if i - distance in devices]
    return lax.ppermute(block, axis, route)


def swap(block, axis, bit):
    n = lax.axis_size(axis)
    return lax.ppermute(block, axis, [(i, i ^ bit) for i in range(n)])


def shards(tokens, norm_gain, expert_ids, gate_weights, w_up, w_down):
    segments = lax.axis_size("section")
    n_exp = lax.axis_size("expert")
    segment_pos = lax.axis_index("section")
    t_pos = lax.axis_index("tensor")
    x_lo = t_pos // 2
    core = t_pos % 2
    micro = tokens.shape[0]
    rows_here = tokens.shape[1]
    quarter = tokens.shape[2]
    capacity = max(3 * rows_here // 8, 2 * rows_here // EXPERTS)
    gain = norm_gain[0]
    gain_from = [gain, swap(gain, "tensor", 1), swap(gain, "tensor", 2), swap(gain, "tensor", 3)]
    gain_full = jnp.concatenate(
        [
            jnp.where(t_pos == q, gain_from[0],
                      jnp.where(t_pos ^ 1 == q, gain_from[1],
                                jnp.where(t_pos ^ 2 == q, gain_from[2], gain_from[3])))
            for q in range(4)
        ]
    )
    up_local = w_up[0]
    down_local = w_down[0]
    local_count = up_local.shape[0]
    copies = n_exp * local_count // EXPERTS
    collected = jnp.zeros((micro, rows_here, quarter), jnp.bfloat16)
    total_steps = micro + segments - 1
    x_first = x_lo == 0
    core_first = core == 0

    def to_half(own, other):
        return jnp.where(
            x_first,
            jnp.concatenate([own, other], axis=-1),
            jnp.concatenate([other, own], axis=-1),
        )

    tokens_half = to_half(tokens, swap(tokens, "tensor", 2))
    routes_all = expert_ids[0].reshape(micro, -1)
    onehot_all = (routes_all[..., None] == jnp.arange(EXPERTS, dtype=jnp.int32)).astype(jnp.int32)
    slot_all = jnp.sum((jnp.cumsum(onehot_all, axis=1) - onehot_all) * onehot_all, axis=2)
    dest_all = routes_all * capacity + slot_all
    source_all = jnp.stack(
        [
            jnp.full((EXPERTS * capacity,), -1, jnp.int32)
            .at[dest_all[m]]
            .set(jnp.arange(2 * rows_here, dtype=jnp.int32) // 2)
            for m in range(micro)
        ]
    )
    n_t = lax.axis_size("tensor")
    cross_route = [
        (s * n_t + t, (s + 1) * n_t + (t ^ 2)) for s in range(segments - 1) for t in range(n_t)
    ]
    def layer_step(step, carried, collected):
        which = step - segment_pos
        which_safe = jnp.clip(which, 0, micro - 1)
        entering = lax.dynamic_index_in_dim(
            tokens_half, jnp.minimum(step, micro - 1), 0, keepdims=False
        )
        half_rows = jnp.where(segment_pos == 0, entering, carried)
        weights = lax.dynamic_index_in_dim(gate_weights[0], which_safe, 0, keepdims=False)
        dest = lax.dynamic_index_in_dim(dest_all, which_safe, 0, keepdims=False)
        source = lax.dynamic_index_in_dim(source_all, which_safe, 0, keepdims=False)
        filled = source >= 0
        outgoing = jnp.where(
            filled[:, None],
            jnp.take(half_rows, jnp.maximum(source, 0), axis=0),
            jnp.zeros((), jnp.bfloat16),
        )
        outgoing = outgoing.reshape(EXPERTS, capacity, 2 * quarter)
        outgoing = jnp.repeat(outgoing, copies, axis=0).reshape(
            n_exp, local_count, capacity, 2 * quarter
        )
        mine = lax.all_to_all(outgoing, "expert", split_axis=0, concat_axis=0, tiled=True)
        def expert_rows(mine):
            theirs = swap(mine, "tensor", 1)
            lo_q = lambda a: a[..., :quarter]
            hi_q = lambda a: a[..., quarter:]
            first = jnp.where(core_first, mine, theirs)
            second = jnp.where(core_first, theirs, mine)
            rows = jnp.concatenate([lo_q(first), lo_q(second), hi_q(first), hi_q(second)], axis=-1)
            rf = rows.astype(jnp.float32)
            sums = jnp.sum(rf * rf, axis=-1)
            normed = (rf * lax.rsqrt(sums / D + 1e-05)[..., None] * gain_full).astype(jnp.bfloat16)
            summed_up = jnp.einsum(
                "sekd,edf->sekf", normed, up_local, preferred_element_type=jnp.float32
            )
            hidden = jax.nn.silu(summed_up).astype(jnp.bfloat16)
            partial_out = jnp.einsum(
                "sekf,efd->sekd", hidden, down_local, preferred_element_type=jnp.float32
            ).astype(jnp.bfloat16)
            pq = [partial_out[..., q * quarter:(q + 1) * quarter] for q in range(4)]
            keep = jnp.where(
                core_first,
                jnp.concatenate([pq[0], pq[2]], axis=-1),
                jnp.concatenate([pq[1], pq[3]], axis=-1),
            )
            give = jnp.where(
                core_first,
                jnp.concatenate([pq[1], pq[3]], axis=-1),
                jnp.concatenate([pq[0], pq[2]], axis=-1),
            )
            got = swap(give, "tensor", 1)
            chip_sum = (keep.astype(jnp.float32) + got.astype(jnp.float32)).astype(jnp.bfloat16)
            return chip_sum

        half_src = n_exp // 2
        chip_sum = jnp.concatenate(
            [expert_rows(mine[:half_src]), expert_rows(mine[half_src:])], axis=0
        )
        returned = lax.all_to_all(chip_sum, "expert", split_axis=0, concat_axis=0, tiled=True)
        summed = jnp.sum(
            returned.reshape(EXPERTS, copies, capacity, 2 * quarter).astype(jnp.float32), axis=1
        )
        picked = jnp.take(summed.reshape(-1, 2 * quarter), dest, axis=0)
        picked = picked.reshape(rows_here, 2, 2 * quarter)
        y_half = jnp.sum(picked * weights[:, :, None], axis=1)
        y_keep = jnp.where(x_first, y_half[:, :quarter], y_half[:, quarter:])
        y_give = jnp.where(x_first, y_half[:, quarter:], y_half[:, :quarter])
        y_got = swap(y_give.astype(jnp.bfloat16), "tensor", 2).astype(jnp.float32)
        xf = jnp.where(x_first, half_rows[:, :quarter], half_rows[:, quarter:]).astype(jnp.float32)
        mixed = xf + (y_keep + y_got)
        produced = mixed.astype(jnp.bfloat16)
        chosen = (jnp.arange(micro, dtype=jnp.int32) == which)[:, None, None]
        collected = jnp.where(chosen, produced[None], collected)
        return produced, collected

    def looped(step, state):
        carried, collected = state
        produced, collected = layer_step(step, carried, collected)
        carried = to_half(
            from_behind(produced, "section", 1),
            lax.ppermute(produced, ("section", "tensor"), cross_route),
        )
        return carried, collected

    carried = jnp.zeros((rows_here, 2 * quarter), jnp.bfloat16)
    carried, collected = lax.fori_loop(0, total_steps - 1, looped, (carried, collected))
    _, collected = layer_step(total_steps - 1, carried, collected)
    return collected[None]


def solution(mesh):
    placed = (
        P(None, "expert", "tensor"),
        P("section", "tensor"),
        P("section", None, "expert", None),
        P("section", None, "expert", None),
        P("section", "expert", None, "tensor"),
        P("section", "expert", "tensor", None),
    )
    return jax.shard_map(
        shards,
        mesh=mesh,
        in_specs=placed,
        out_specs=P("section", None, "expert", "tensor"),
        check_vma=False,
    )
```

```python
import jax
import jax.numpy as jnp
from jax import lax
from jax.sharding import PartitionSpec as P

D = 3072
EXPERTS = 8


def from_behind(block, axis, distance):
    devices = range(lax.axis_size(axis))
    route = [(i - distance, i) for i in devices if i - distance in devices]
    return lax.ppermute(block, axis, route)


def swap(block, axis, bit):
    n = lax.axis_size(axis)
    return lax.ppermute(block, axis, [(i, i ^ bit) for i in range(n)])


def shards(tokens, norm_gain, expert_ids, gate_weights, w_up, w_down):
    segments = lax.axis_size("section")
    n_exp = lax.axis_size("expert")
    segment_pos = lax.axis_index("section")
    t_pos = lax.axis_index("tensor")
    x_lo = t_pos // 2
    core = t_pos % 2
    micro = tokens.shape[0]
    rows_here = tokens.shape[1]
    quarter = tokens.shape[2]
    capacity = max(3 * rows_here // 8, 2 * rows_here // EXPERTS)
    gain = norm_gain[0]
    gain_from = [gain, swap(gain, "tensor", 1), swap(gain, "tensor", 2), swap(gain, "tensor", 3)]
    gain_full = jnp.concatenate(
        [
            jnp.where(t_pos == q, gain_from[0],
                      jnp.where(t_pos ^ 1 == q, gain_from[1],
                                jnp.where(t_pos ^ 2 == q, gain_from[2], gain_from[3])))
            for q in range(4)
        ]
    )
    up_local = w_up[0]
    down_local = w_down[0]
    local_count = up_local.shape[0]
    copies = n_exp * local_count // EXPERTS
    collected = jnp.zeros((micro, rows_here, quarter), jnp.bfloat16)
    total_steps = micro + segments - 1
    x_first = x_lo == 0
    core_first = core == 0

    def to_half(own, other):
        return jnp.where(
            x_first,
            jnp.concatenate([own, other], axis=-1),
            jnp.concatenate([other, own], axis=-1),
        )

    tokens_half = to_half(tokens, swap(tokens, "tensor", 2))
    routes_all = expert_ids[0].reshape(micro, -1)
    onehot_all = (routes_all[..., None] == jnp.arange(EXPERTS, dtype=jnp.int32)).astype(jnp.int32)
    slot_all = jnp.sum((jnp.cumsum(onehot_all, axis=1) - onehot_all) * onehot_all, axis=2)
    dest_all = routes_all * capacity + slot_all
    source_all = jnp.stack(
        [
            jnp.full((EXPERTS * capacity,), -1, jnp.int32)
            .at[dest_all[m]]
            .set(jnp.arange(2 * rows_here, dtype=jnp.int32) // 2)
            for m in range(micro)
        ]
    )
    n_t = lax.axis_size("tensor")
    cross_route = [
        (s * n_t + t, (s + 1) * n_t + (t ^ 2)) for s in range(segments - 1) for t in range(n_t)
    ]
    def layer_step(step, carried, collected):
        which = step - segment_pos
        which_safe = jnp.clip(which, 0, micro - 1)
        entering = lax.dynamic_index_in_dim(
            tokens_half, jnp.minimum(step, micro - 1), 0, keepdims=False
        )
        half_rows = jnp.where(segment_pos == 0, entering, carried)
        weights = lax.dynamic_index_in_dim(gate_weights[0], which_safe, 0, keepdims=False)
        dest = lax.dynamic_index_in_dim(dest_all, which_safe, 0, keepdims=False)
        source = lax.dynamic_index_in_dim(source_all, which_safe, 0, keepdims=False)
        filled = source >= 0
        outgoing = jnp.where(
            filled[:, None],
            jnp.take(half_rows, jnp.maximum(source, 0), axis=0),
            jnp.zeros((), jnp.bfloat16),
        )
        outgoing = outgoing.reshape(EXPERTS, capacity, 2 * quarter)
        outgoing = jnp.repeat(outgoing, copies, axis=0).reshape(
            n_exp, local_count, capacity, 2 * quarter
        )
        mine = lax.all_to_all(outgoing, "expert", split_axis=0, concat_axis=0, tiled=True)
        theirs = swap(mine, "tensor", 1)
        lo_q = lambda a: a[..., :quarter]
        hi_q = lambda a: a[..., quarter:]
        first = jnp.where(core_first, mine, theirs)
        second = jnp.where(core_first, theirs, mine)
        rows = jnp.concatenate(
            [lo_q(first), lo_q(second), hi_q(first), hi_q(second)], axis=-1
        ).reshape(-1, D)
        rf = rows.astype(jnp.float32)
        sums = jnp.sum(rf * rf, axis=-1)
        normed = (rf * lax.rsqrt(sums / D + 1e-05)[..., None] * gain_full).astype(jnp.bfloat16)
        summed_up = jnp.dot(normed, up_local[0], preferred_element_type=jnp.float32)
        hidden = jax.nn.silu(summed_up).astype(jnp.bfloat16)
        partial_out = jnp.dot(
            hidden, down_local[0], preferred_element_type=jnp.float32
        ).astype(jnp.bfloat16)
        pq = [partial_out[..., q * quarter:(q + 1) * quarter] for q in range(4)]
        keep = jnp.where(
            core_first,
            jnp.concatenate([pq[0], pq[2]], axis=-1),
            jnp.concatenate([pq[1], pq[3]], axis=-1),
        )
        give = jnp.where(
            core_first,
            jnp.concatenate([pq[1], pq[3]], axis=-1),
            jnp.concatenate([pq[0], pq[2]], axis=-1),
        )
        got = swap(give, "tensor", 1)
        chip_sum = (keep.astype(jnp.float32) + got.astype(jnp.float32)).astype(jnp.bfloat16)
        chip_sum = chip_sum.reshape(mine.shape)
        returned = lax.all_to_all(chip_sum, "expert", split_axis=0, concat_axis=0, tiled=True)
        summed = jnp.sum(
            returned.reshape(EXPERTS, copies, capacity, 2 * quarter).astype(jnp.float32), axis=1
        )
        picked = jnp.take(summed.reshape(-1, 2 * quarter), dest, axis=0)
        picked = picked.reshape(rows_here, 2, 2 * quarter)
        y_half = jnp.sum(picked * weights[:, :, None], axis=1)
        y_keep = jnp.where(x_first, y_half[:, :quarter], y_half[:, quarter:])
        y_give = jnp.where(x_first, y_half[:, quarter:], y_half[:, :quarter])
        y_got = swap(y_give.astype(jnp.bfloat16), "tensor", 2).astype(jnp.float32)
        xf = jnp.where(x_first, half_rows[:, :quarter], half_rows[:, quarter:]).astype(jnp.float32)
        mixed = xf + (y_keep + y_got)
        produced = mixed.astype(jnp.bfloat16)
        chosen = (jnp.arange(micro, dtype=jnp.int32) == which)[:, None, None]
        collected = jnp.where(chosen, produced[None], collected)
        return produced, collected

    def looped(step, state):
        carried, collected = state
        produced, collected = layer_step(step, carried, collected)
        carried = to_half(
            from_behind(produced, "section", 1),
            lax.ppermute(produced, ("section", "tensor"), cross_route),
        )
        return carried, collected

    carried = jnp.zeros((rows_here, 2 * quarter), jnp.bfloat16)
    carried, collected = lax.fori_loop(0, total_steps - 1, looped, (carried, collected))
    _, collected = layer_step(total_steps - 1, carried, collected)
    return collected[None]


def solution(mesh):
    placed = (
        P(None, "expert", "tensor"),
        P("section", "tensor"),
        P("section", None, "expert", None),
        P("section", None, "expert", None),
        P("section", "expert", None, "tensor"),
        P("section", "expert", "tensor", None),
    )
    return jax.shard_map(
        shards,
        mesh=mesh,
        in_specs=placed,
        out_specs=P("section", None, "expert", "tensor"),
        check_vma=False,
    )
```

```python
import jax
import jax.numpy as jnp
from jax import lax
from jax.sharding import PartitionSpec as P

D = 3072
EXPERTS = 8


def from_behind(block, axis, distance):
    devices = range(lax.axis_size(axis))
    route = [(i - distance, i) for i in devices if i - distance in devices]
    return lax.ppermute(block, axis, route)


def swap(block, axis, bit):
    n = lax.axis_size(axis)
    return lax.ppermute(block, axis, [(i, i ^ bit) for i in range(n)])


def shards(tokens, norm_gain, expert_ids, gate_weights, w_up, w_down):
    segments = lax.axis_size("section")
    n_exp = lax.axis_size("expert")
    segment_pos = lax.axis_index("section")
    t_pos = lax.axis_index("tensor")
    x_lo = t_pos // 2
    core = t_pos % 2
    micro = tokens.shape[0]
    rows_here = tokens.shape[1]
    quarter = tokens.shape[2]
    capacity = max(3 * rows_here // 8, 2 * rows_here // EXPERTS)
    gain = norm_gain[0]
    gain_from = [gain, swap(gain, "tensor", 1), swap(gain, "tensor", 2), swap(gain, "tensor", 3)]
    gain_full = jnp.concatenate(
        [
            jnp.where(t_pos == q, gain_from[0],
                      jnp.where(t_pos ^ 1 == q, gain_from[1],
                                jnp.where(t_pos ^ 2 == q, gain_from[2], gain_from[3])))
            for q in range(4)
        ]
    )
    up_local = w_up[0]
    down_local = w_down[0]
    local_count = up_local.shape[0]
    copies = n_exp * local_count // EXPERTS
    collected = jnp.zeros((micro, rows_here, quarter), jnp.bfloat16)
    total_steps = micro + segments - 1
    x_first = x_lo == 0
    core_first = core == 0

    def to_half(own, other):
        return jnp.where(
            x_first,
            jnp.concatenate([own, other], axis=-1),
            jnp.concatenate([other, own], axis=-1),
        )

    tokens_half = jnp.stack(
        [to_half(tokens[m], swap(tokens[m], "tensor", 2)) for m in range(micro)]
    )
    routes_all = expert_ids[0].reshape(micro, -1)
    onehot_all = (routes_all[..., None] == jnp.arange(EXPERTS, dtype=jnp.int32)).astype(jnp.int32)
    slot_all = jnp.sum((jnp.cumsum(onehot_all, axis=1) - onehot_all) * onehot_all, axis=2)
    dest_all = routes_all * capacity + slot_all
    source_all = jnp.stack(
        [
            jnp.full((EXPERTS * capacity,), -1, jnp.int32)
            .at[dest_all[m]]
            .set(jnp.arange(2 * rows_here, dtype=jnp.int32) // 2)
            for m in range(micro)
        ]
    )
    n_t = lax.axis_size("tensor")
    cross_route = [
        (s * n_t + t, (s + 1) * n_t + (t ^ 2)) for s in range(segments - 1) for t in range(n_t)
    ]
    def layer_step(step, carried, collected):
        which = step - segment_pos
        which_safe = jnp.clip(which, 0, micro - 1)
        entering = lax.dynamic_index_in_dim(
            tokens_half, jnp.minimum(step, micro - 1), 0, keepdims=False
        )
        half_rows = jnp.where(segment_pos == 0, entering, carried)
        weights = lax.dynamic_index_in_dim(gate_weights[0], which_safe, 0, keepdims=False)
        dest = lax.dynamic_index_in_dim(dest_all, which_safe, 0, keepdims=False)
        source = lax.dynamic_index_in_dim(source_all, which_safe, 0, keepdims=False)
        filled = source >= 0
        outgoing = jnp.where(
            filled[:, None],
            jnp.take(half_rows, jnp.maximum(source, 0), axis=0),
            jnp.zeros((), jnp.bfloat16),
        )
        outgoing = outgoing.reshape(EXPERTS, capacity, 2 * quarter)
        outgoing = jnp.repeat(outgoing, copies, axis=0).reshape(
            n_exp, local_count, capacity, 2 * quarter
        )
        mine = lax.all_to_all(outgoing, "expert", split_axis=0, concat_axis=0, tiled=True)
        theirs = swap(mine, "tensor", 1)
        lo_q = lambda a: a[..., :quarter]
        hi_q = lambda a: a[..., quarter:]
        first = jnp.where(core_first, mine, theirs)
        second = jnp.where(core_first, theirs, mine)
        rows = jnp.concatenate([lo_q(first), lo_q(second), hi_q(first), hi_q(second)], axis=-1)
        rf = rows.astype(jnp.float32)
        sums = jnp.sum(rf * rf, axis=-1)
        normed = (rf * lax.rsqrt(sums / D + 1e-05)[..., None] * gain_full).astype(jnp.bfloat16)
        summed_up = jnp.einsum(
            "sekd,edf->sekf", normed, up_local, preferred_element_type=jnp.float32
        )
        hidden = jax.nn.silu(summed_up).astype(jnp.bfloat16)
        partial_out = jnp.einsum(
            "sekf,efd->sekd", hidden, down_local, preferred_element_type=jnp.float32
        )
        pq = [partial_out[..., q * quarter:(q + 1) * quarter] for q in range(4)]
        keep = jnp.where(
            core_first,
            jnp.concatenate([pq[0], pq[2]], axis=-1),
            jnp.concatenate([pq[1], pq[3]], axis=-1),
        )
        give = jnp.where(
            core_first,
            jnp.concatenate([pq[1], pq[3]], axis=-1),
            jnp.concatenate([pq[0], pq[2]], axis=-1),
        )
        got = swap(give.astype(jnp.bfloat16), "tensor", 1)
        chip_sum = (keep + got.astype(jnp.float32)).astype(jnp.bfloat16)
        returned = lax.all_to_all(chip_sum, "expert", split_axis=0, concat_axis=0, tiled=True)
        summed = jnp.sum(
            returned.reshape(EXPERTS, copies, capacity, 2 * quarter).astype(jnp.float32), axis=1
        )
        picked = jnp.take(summed.reshape(-1, 2 * quarter), dest, axis=0)
        picked = picked.reshape(rows_here, 2, 2 * quarter)
        y_half = jnp.sum(picked * weights[:, :, None], axis=1)
        y_keep = jnp.where(x_first, y_half[:, :quarter], y_half[:, quarter:])
        y_give = jnp.where(x_first, y_half[:, quarter:], y_half[:, :quarter])
        y_got = swap(y_give.astype(jnp.bfloat16), "tensor", 2).astype(jnp.float32)
        xf = jnp.where(x_first, half_rows[:, :quarter], half_rows[:, quarter:]).astype(jnp.float32)
        mixed = xf + (y_keep + y_got)
        produced = mixed.astype(jnp.bfloat16)
        chosen = (jnp.arange(micro, dtype=jnp.int32) == which)[:, None, None]
        collected = jnp.where(chosen, produced[None], collected)
        return produced, collected

    def looped(step, state):
        carried, collected = state
        produced, collected = layer_step(step, carried, collected)
        carried = to_half(
            from_behind(produced, "section", 1),
            lax.ppermute(produced, ("section", "tensor"), cross_route),
        )
        return carried, collected

    carried = jnp.zeros((rows_here, 2 * quarter), jnp.bfloat16)
    carried, collected = lax.fori_loop(0, total_steps - 1, looped, (carried, collected))
    _, collected = layer_step(total_steps - 1, carried, collected)
    return collected[None]


def solution(mesh):
    placed = (
        P(None, "expert", "tensor"),
        P("section", "tensor"),
        P("section", None, "expert", None),
        P("section", None, "expert", None),
        P("section", "expert", None, "tensor"),
        P("section", "expert", "tensor", None),
    )
    return jax.shard_map(
        shards,
        mesh=mesh,
        in_specs=placed,
        out_specs=P("section", None, "expert", "tensor"),
        check_vma=False,
    )
```

```python
import jax
import jax.numpy as jnp
from jax import lax
from jax.sharding import PartitionSpec as P

D = 3072
EXPERTS = 8


def from_behind(block, axis, distance):
    devices = range(lax.axis_size(axis))
    route = [(i - distance, i) for i in devices if i - distance in devices]
    return lax.ppermute(block, axis, route)


def swap(block, axis, bit):
    n = lax.axis_size(axis)
    return lax.ppermute(block, axis, [(i, i ^ bit) for i in range(n)])


def shards(tokens, norm_gain, expert_ids, gate_weights, w_up, w_down):
    segments = lax.axis_size("section")
    n_exp = lax.axis_size("expert")
    segment_pos = lax.axis_index("section")
    t_pos = lax.axis_index("tensor")
    x_lo = t_pos // 2
    core = t_pos % 2
    micro = tokens.shape[0]
    rows_here = tokens.shape[1]
    quarter = tokens.shape[2]
    capacity = max(3 * rows_here // 8, 2 * rows_here // EXPERTS)
    gain = norm_gain[0]
    gain_from = [gain, swap(gain, "tensor", 1), swap(gain, "tensor", 2), swap(gain, "tensor", 3)]
    gain_full = jnp.concatenate(
        [
            jnp.where(t_pos == q, gain_from[0],
                      jnp.where(t_pos ^ 1 == q, gain_from[1],
                                jnp.where(t_pos ^ 2 == q, gain_from[2], gain_from[3])))
            for q in range(4)
        ]
    )
    up_local = w_up[0]
    down_local = w_down[0]
    local_count = up_local.shape[0]
    copies = n_exp * local_count // EXPERTS
    collected = jnp.zeros((micro, rows_here, quarter), jnp.bfloat16)
    total_steps = micro + segments - 1
    x_first = x_lo == 0
    core_first = core == 0

    def to_half(own, other):
        return jnp.where(
            x_first,
            jnp.concatenate([own, other], axis=-1),
            jnp.concatenate([other, own], axis=-1),
        )

    tokens_half = to_half(tokens, swap(tokens, "tensor", 2))
    routes_all = expert_ids[0].reshape(micro, -1)
    onehot_all = (routes_all[..., None] == jnp.arange(EXPERTS, dtype=jnp.int32)).astype(jnp.int32)
    slot_all = jnp.sum((jnp.cumsum(onehot_all, axis=1) - onehot_all) * onehot_all, axis=2)
    dest_all = routes_all * capacity + slot_all
    source_all = jnp.stack(
        [
            jnp.full((EXPERTS * capacity,), -1, jnp.int32)
            .at[dest_all[m]]
            .set(jnp.arange(2 * rows_here, dtype=jnp.int32) // 2)
            for m in range(micro)
        ]
    )
    n_t = lax.axis_size("tensor")
    cross_route = [
        (s * n_t + t, (s + 1) * n_t + (t ^ 2)) for s in range(segments - 1) for t in range(n_t)
    ]
    def layer_step(step, carried, collected):
        which = step - segment_pos
        which_safe = jnp.clip(which, 0, micro - 1)
        entering = lax.dynamic_index_in_dim(
            tokens_half, jnp.minimum(step, micro - 1), 0, keepdims=False
        )
        half_rows = jnp.where(segment_pos == 0, entering, carried)
        weights = lax.dynamic_index_in_dim(gate_weights[0], which_safe, 0, keepdims=False)
        dest = lax.dynamic_index_in_dim(dest_all, which_safe, 0, keepdims=False)
        source = lax.dynamic_index_in_dim(source_all, which_safe, 0, keepdims=False)
        filled = source >= 0
        outgoing = jnp.where(
            filled[:, None],
            jnp.take(half_rows, jnp.maximum(source, 0), axis=0),
            jnp.zeros((), jnp.bfloat16),
        )
        outgoing = outgoing.reshape(EXPERTS, capacity, 2 * quarter)
        outgoing = jnp.repeat(outgoing, copies, axis=0).reshape(
            n_exp, local_count, capacity, 2 * quarter
        )
        mine = lax.all_to_all(outgoing, "expert", split_axis=0, concat_axis=0, tiled=True)
        theirs = swap(mine, "tensor", 1)
        lo_q = lambda a: a[..., :quarter]
        hi_q = lambda a: a[..., quarter:]
        first = jnp.where(core_first, mine, theirs)
        second = jnp.where(core_first, theirs, mine)
        rows = jnp.concatenate([lo_q(first), lo_q(second), hi_q(first), hi_q(second)], axis=-1)
        rf = rows.astype(jnp.float32)
        sums = jnp.sum(rf * rf, axis=-1)
        normed = (rf * lax.rsqrt(sums / D + 1e-05)[..., None] * gain_full).astype(jnp.bfloat16)
        summed_up = jnp.einsum(
            "sekd,edf->sekf", normed, up_local, preferred_element_type=jnp.float32
        )
        hidden = jax.nn.silu(summed_up).astype(jnp.bfloat16)
        partial_out = jnp.einsum(
            "sekf,efd->sekd", hidden, down_local, preferred_element_type=jnp.float32
        )
        pq = [partial_out[..., q * quarter:(q + 1) * quarter] for q in range(4)]
        keep = jnp.where(
            core_first,
            jnp.concatenate([pq[0], pq[2]], axis=-1),
            jnp.concatenate([pq[1], pq[3]], axis=-1),
        )
        give = jnp.where(
            core_first,
            jnp.concatenate([pq[1], pq[3]], axis=-1),
            jnp.concatenate([pq[0], pq[2]], axis=-1),
        )
        got = swap(give.astype(jnp.bfloat16), "tensor", 1)
        chip_sum = (keep + got.astype(jnp.float32)).astype(jnp.bfloat16)
        returned = lax.all_to_all(chip_sum, "expert", split_axis=0, concat_axis=0, tiled=True)
        summed = jnp.sum(
            returned.reshape(EXPERTS, copies, capacity, 2 * quarter).astype(jnp.float32), axis=1
        )
        picked = jnp.take(summed.reshape(-1, 2 * quarter), dest, axis=0)
        picked = picked.reshape(rows_here, 2, 2 * quarter)
        y_half = jnp.sum(picked * weights[:, :, None], axis=1)
        y_keep = jnp.where(x_first, y_half[:, :quarter], y_half[:, quarter:])
        y_give = jnp.where(x_first, y_half[:, quarter:], y_half[:, :quarter])
        y_got = swap(y_give.astype(jnp.bfloat16), "tensor", 2).astype(jnp.float32)
        xf = jnp.where(x_first, half_rows[:, :quarter], half_rows[:, quarter:]).astype(jnp.float32)
        mixed = xf + (y_keep + y_got)
        produced = mixed.astype(jnp.bfloat16)
        chosen = (jnp.arange(micro, dtype=jnp.int32) == which)[:, None, None]
        collected = jnp.where(chosen, produced[None], collected)
        return produced, collected

    def looped(step, state):
        carried, collected = state
        produced, collected = layer_step(step, carried, collected)
        carried = to_half(
            from_behind(produced, "section", 1),
            lax.ppermute(produced, ("section", "tensor"), cross_route),
        )
        return carried, collected

    carried = jnp.zeros((rows_here, 2 * quarter), jnp.bfloat16)
    carried, collected = lax.fori_loop(0, total_steps - 1, looped, (carried, collected))
    _, collected = layer_step(total_steps - 1, carried, collected)
    return collected[None]


def solution(mesh):
    placed = (
        P(None, "expert", "tensor"),
        P("section", "tensor"),
        P("section", None, "expert", None),
        P("section", None, "expert", None),
        P("section", "expert", None, "tensor"),
        P("section", "expert", "tensor", None),
    )
    return jax.shard_map(
        shards,
        mesh=mesh,
        in_specs=placed,
        out_specs=P("section", None, "expert", "tensor"),
        check_vma=False,
    )
```

```python
import jax
import jax.numpy as jnp
from jax import lax
from jax.sharding import PartitionSpec as P

D = 3072
EXPERTS = 8


def from_behind(block, axis, distance):
    devices = range(lax.axis_size(axis))
    route = [(i - distance, i) for i in devices if i - distance in devices]
    return lax.ppermute(block, axis, route)


def swap(block, axis, bit):
    n = lax.axis_size(axis)
    return lax.ppermute(block, axis, [(i, i ^ bit) for i in range(n)])


def shards(tokens, norm_gain, expert_ids, gate_weights, w_up, w_down):
    segments = lax.axis_size("section")
    n_exp = lax.axis_size("expert")
    segment_pos = lax.axis_index("section")
    t_pos = lax.axis_index("tensor")
    x_lo = t_pos // 2
    core = t_pos % 2
    micro = tokens.shape[0]
    rows_here = tokens.shape[1]
    quarter = tokens.shape[2]
    capacity = max(3 * rows_here // 8, 2 * rows_here // EXPERTS)
    gain = norm_gain[0]
    gain_from = [gain, swap(gain, "tensor", 1), swap(gain, "tensor", 2), swap(gain, "tensor", 3)]
    gain_full = jnp.concatenate(
        [
            jnp.where(t_pos == q, gain_from[0],
                      jnp.where(t_pos ^ 1 == q, gain_from[1],
                                jnp.where(t_pos ^ 2 == q, gain_from[2], gain_from[3])))
            for q in range(4)
        ]
    )
    up_local = w_up[0]
    down_local = w_down[0]
    local_count = up_local.shape[0]
    copies = n_exp * local_count // EXPERTS
    collected = jnp.zeros((micro, rows_here, quarter), jnp.bfloat16)
    total_steps = micro + segments - 1
    x_first = x_lo == 0
    core_first = core == 0

    def to_half(own, other):
        return jnp.where(
            x_first,
            jnp.concatenate([own, other], axis=-1),
            jnp.concatenate([other, own], axis=-1),
        )

    tokens_half = to_half(tokens, swap(tokens, "tensor", 2))
    routes_all = expert_ids[0].reshape(micro, -1)
    onehot_all = (routes_all[..., None] == jnp.arange(EXPERTS, dtype=jnp.int32)).astype(jnp.int32)
    slot_all = jnp.sum((jnp.cumsum(onehot_all, axis=1) - onehot_all) * onehot_all, axis=2)
    dest_all = routes_all * capacity + slot_all
    source_all = jnp.stack(
        [
            jnp.full((EXPERTS * capacity,), -1, jnp.int32)
            .at[dest_all[m]]
            .set(jnp.arange(2 * rows_here, dtype=jnp.int32) // 2)
            for m in range(micro)
        ]
    )
    n_t = lax.axis_size("tensor")
    cross_route = [
        (s * n_t + t, (s + 1) * n_t + (t ^ 2)) for s in range(segments - 1) for t in range(n_t)
    ]
    def layer_step(step, carried, collected):
        which = step - segment_pos
        which_safe = jnp.clip(which, 0, micro - 1)
        entering = lax.dynamic_index_in_dim(
            tokens_half, jnp.minimum(step, micro - 1), 0, keepdims=False
        )
        half_rows = jnp.where(segment_pos == 0, entering, carried)
        weights = lax.dynamic_index_in_dim(gate_weights[0], which_safe, 0, keepdims=False)
        dest = lax.dynamic_index_in_dim(dest_all, which_safe, 0, keepdims=False)
        source = lax.dynamic_index_in_dim(source_all, which_safe, 0, keepdims=False)
        filled = source >= 0
        outgoing = jnp.where(
            filled[:, None],
            jnp.take(half_rows, jnp.maximum(source, 0), axis=0),
            jnp.zeros((), jnp.bfloat16),
        )
        outgoing = outgoing.reshape(EXPERTS, capacity, 2 * quarter)
        outgoing = jnp.repeat(outgoing, copies, axis=0).reshape(
            n_exp, local_count, capacity, 2 * quarter
        )
        mine = lax.all_to_all(outgoing, "expert", split_axis=0, concat_axis=0, tiled=True)
        theirs = swap(mine, "tensor", 1)
        lo_q = lambda a: a[..., :quarter]
        hi_q = lambda a: a[..., quarter:]
        first = jnp.where(core_first, mine, theirs)
        second = jnp.where(core_first, theirs, mine)
        rows = jnp.concatenate([lo_q(first), lo_q(second), hi_q(first), hi_q(second)], axis=-1)
        rf = rows.astype(jnp.float32)
        sums = jnp.sum(rf * rf, axis=-1)
        normed = (rf * lax.rsqrt(sums / D + 1e-05)[..., None] * gain_full).astype(jnp.bfloat16)
        summed_up = jnp.einsum(
            "sekd,edf->sekf", normed, up_local, preferred_element_type=jnp.float32
        )
        hidden = jax.nn.silu(summed_up).astype(jnp.bfloat16)
        partial_out = jnp.einsum(
            "sekf,efd->sekd", hidden, down_local, preferred_element_type=jnp.float32
        )
        pq = [partial_out[..., q * quarter:(q + 1) * quarter] for q in range(4)]
        keep = jnp.where(
            core_first,
            jnp.concatenate([pq[0], pq[2]], axis=-1),
            jnp.concatenate([pq[1], pq[3]], axis=-1),
        )
        give = jnp.where(
            core_first,
            jnp.concatenate([pq[1], pq[3]], axis=-1),
            jnp.concatenate([pq[0], pq[2]], axis=-1),
        )
        got = swap(give.astype(jnp.bfloat16), "tensor", 1)
        chip_sum = (keep + got.astype(jnp.float32)).astype(jnp.bfloat16)
        returned = lax.all_to_all(chip_sum, "expert", split_axis=0, concat_axis=0, tiled=True)
        summed = jnp.sum(
            returned.reshape(EXPERTS, copies, capacity, 2 * quarter).astype(jnp.float32), axis=1
        )
        picked = jnp.take(summed.reshape(-1, 2 * quarter), dest, axis=0)
        picked = picked.reshape(rows_here, 2, 2 * quarter)
        y_half = jnp.sum(picked * weights[:, :, None], axis=1)
        y_mine = y_half.astype(jnp.bfloat16)
        y_other = swap(y_mine, "tensor", 2)
        full_half = (
            half_rows.astype(jnp.float32)
            + (y_mine.astype(jnp.float32) + y_other.astype(jnp.float32))
        ).astype(jnp.bfloat16)
        produced = jnp.where(x_first, full_half[:, :quarter], full_half[:, quarter:])
        chosen = (jnp.arange(micro, dtype=jnp.int32) == which)[:, None, None]
        collected = jnp.where(chosen, produced[None], collected)
        return full_half, collected

    def looped(step, state):
        carried, collected = state
        full_half, collected = layer_step(step, carried, collected)
        carried = lax.ppermute(full_half, ("section", "tensor"), cross_route)
        return carried, collected

    carried = jnp.zeros((rows_here, 2 * quarter), jnp.bfloat16)
    carried, collected = lax.fori_loop(0, total_steps - 1, looped, (carried, collected))
    _, collected = layer_step(total_steps - 1, carried, collected)
    return collected[None]


def solution(mesh):
    placed = (
        P(None, "expert", "tensor"),
        P("section", "tensor"),
        P("section", None, "expert", None),
        P("section", None, "expert", None),
        P("section", "expert", None, "tensor"),
        P("section", "expert", "tensor", None),
    )
    return jax.shard_map(
        shards,
        mesh=mesh,
        in_specs=placed,
        out_specs=P("section", None, "expert", "tensor"),
        check_vma=False,
    )
```

```python
import jax
import jax.numpy as jnp
from jax import lax
from jax.sharding import PartitionSpec as P

D = 3072
EXPERTS = 8


def from_behind(block, axis, distance):
    devices = range(lax.axis_size(axis))
    route = [(i - distance, i) for i in devices if i - distance in devices]
    return lax.ppermute(block, axis, route)


def swap(block, axis, bit):
    n = lax.axis_size(axis)
    return lax.ppermute(block, axis, [(i, i ^ bit) for i in range(n)])


def shards(tokens, norm_gain, expert_ids, gate_weights, w_up, w_down):
    segments = lax.axis_size("section")
    n_exp = lax.axis_size("expert")
    segment_pos = lax.axis_index("section")
    t_pos = lax.axis_index("tensor")
    x_lo = t_pos // 2
    core = t_pos % 2
    micro = tokens.shape[0]
    rows_here = tokens.shape[1]
    quarter = tokens.shape[2]
    capacity = max(3 * rows_here // 8, 2 * rows_here // EXPERTS)
    gain = norm_gain[0]
    gain_from = [gain, swap(gain, "tensor", 1), swap(gain, "tensor", 2), swap(gain, "tensor", 3)]
    gain_full = jnp.concatenate(
        [
            jnp.where(t_pos == q, gain_from[0],
                      jnp.where(t_pos ^ 1 == q, gain_from[1],
                                jnp.where(t_pos ^ 2 == q, gain_from[2], gain_from[3])))
            for q in range(4)
        ]
    )
    up_local = w_up[0]
    down_local = w_down[0]
    local_count = up_local.shape[0]
    copies = n_exp * local_count // EXPERTS
    collected = jnp.zeros((micro, rows_here, quarter), jnp.bfloat16)
    total_steps = micro + segments - 1
    x_first = x_lo == 0
    core_first = core == 0

    def to_half(own, other):
        return jnp.where(
            x_first,
            jnp.concatenate([own, other], axis=-1),
            jnp.concatenate([other, own], axis=-1),
        )

    tokens_half = to_half(tokens, swap(tokens, "tensor", 2))
    routes_all = expert_ids[0].reshape(micro, -1)
    onehot_all = (routes_all[..., None] == jnp.arange(EXPERTS, dtype=jnp.int32)).astype(jnp.int32)
    slot_all = jnp.sum((jnp.cumsum(onehot_all, axis=1) - onehot_all) * onehot_all, axis=2)
    dest_all = routes_all * capacity + slot_all
    source_all = jnp.stack(
        [
            jnp.full((EXPERTS * capacity,), -1, jnp.int32)
            .at[dest_all[m]]
            .set(jnp.arange(2 * rows_here, dtype=jnp.int32) // 2)
            for m in range(micro)
        ]
    )
    n_t = lax.axis_size("tensor")
    cross_route = [
        (s * n_t + t, ((s + 1) % segments) * n_t + (t ^ 2)) for s in range(segments) for t in range(n_t)
    ]
    def layer_step(step, carried, collected):
        which = step - segment_pos
        which_safe = jnp.clip(which, 0, micro - 1)
        entering = lax.dynamic_index_in_dim(
            tokens_half, jnp.minimum(step, micro - 1), 0, keepdims=False
        )
        half_rows = jnp.where(segment_pos == 0, entering, carried)
        weights = lax.dynamic_index_in_dim(gate_weights[0], which_safe, 0, keepdims=False)
        dest = lax.dynamic_index_in_dim(dest_all, which_safe, 0, keepdims=False)
        source = lax.dynamic_index_in_dim(source_all, which_safe, 0, keepdims=False)
        filled = source >= 0
        outgoing = jnp.where(
            filled[:, None],
            jnp.take(half_rows, jnp.maximum(source, 0), axis=0),
            jnp.zeros((), jnp.bfloat16),
        )
        outgoing = outgoing.reshape(EXPERTS, capacity, 2 * quarter)
        outgoing = jnp.repeat(outgoing, copies, axis=0).reshape(
            n_exp, local_count, capacity, 2 * quarter
        )
        mine = lax.all_to_all(outgoing, "expert", split_axis=0, concat_axis=0, tiled=True)
        theirs = swap(mine, "tensor", 1)
        lo_q = lambda a: a[..., :quarter]
        hi_q = lambda a: a[..., quarter:]
        first = jnp.where(core_first, mine, theirs)
        second = jnp.where(core_first, theirs, mine)
        rows = jnp.concatenate([lo_q(first), lo_q(second), hi_q(first), hi_q(second)], axis=-1)
        rf = rows.astype(jnp.float32)
        sums = jnp.sum(rf * rf, axis=-1)
        normed = (rf * lax.rsqrt(sums / D + 1e-05)[..., None] * gain_full).astype(jnp.bfloat16)
        summed_up = jnp.einsum(
            "sekd,edf->sekf", normed, up_local, preferred_element_type=jnp.float32
        )
        hidden = jax.nn.silu(summed_up).astype(jnp.bfloat16)
        partial_out = jnp.einsum(
            "sekf,efd->sekd", hidden, down_local, preferred_element_type=jnp.float32
        )
        pq = [partial_out[..., q * quarter:(q + 1) * quarter] for q in range(4)]
        keep = jnp.where(
            core_first,
            jnp.concatenate([pq[0], pq[2]], axis=-1),
            jnp.concatenate([pq[1], pq[3]], axis=-1),
        )
        give = jnp.where(
            core_first,
            jnp.concatenate([pq[1], pq[3]], axis=-1),
            jnp.concatenate([pq[0], pq[2]], axis=-1),
        )
        got = swap(give.astype(jnp.bfloat16), "tensor", 1)
        chip_sum = (keep + got.astype(jnp.float32)).astype(jnp.bfloat16)
        returned = lax.all_to_all(chip_sum, "expert", split_axis=0, concat_axis=0, tiled=True)
        summed = jnp.sum(
            returned.reshape(EXPERTS, copies, capacity, 2 * quarter).astype(jnp.float32), axis=1
        )
        picked = jnp.take(summed.reshape(-1, 2 * quarter), dest, axis=0)
        picked = picked.reshape(rows_here, 2, 2 * quarter)
        y_half = jnp.sum(picked * weights[:, :, None], axis=1)
        y_keep = jnp.where(x_first, y_half[:, :quarter], y_half[:, quarter:])
        y_give = jnp.where(x_first, y_half[:, quarter:], y_half[:, :quarter])
        y_got = swap(y_give.astype(jnp.bfloat16), "tensor", 2).astype(jnp.float32)
        xf = jnp.where(x_first, half_rows[:, :quarter], half_rows[:, quarter:]).astype(jnp.float32)
        mixed = xf + (y_keep + y_got)
        produced = mixed.astype(jnp.bfloat16)
        chosen = (jnp.arange(micro, dtype=jnp.int32) == which)[:, None, None]
        collected = jnp.where(chosen, produced[None], collected)
        return produced, collected

    def looped(step, state):
        carried, collected = state
        produced, collected = layer_step(step, carried, collected)
        carried = to_half(
            lax.ppermute(produced, "section", [(i, (i + 1) % segments) for i in range(segments)]),
            lax.ppermute(produced, ("section", "tensor"), cross_route),
        )
        return carried, collected

    carried = jnp.zeros((rows_here, 2 * quarter), jnp.bfloat16)
    carried, collected = lax.fori_loop(0, total_steps - 1, looped, (carried, collected))
    _, collected = layer_step(total_steps - 1, carried, collected)
    return collected[None]


def solution(mesh):
    placed = (
        P(None, "expert", "tensor"),
        P("section", "tensor"),
        P("section", None, "expert", None),
        P("section", None, "expert", None),
        P("section", "expert", None, "tensor"),
        P("section", "expert", "tensor", None),
    )
    return jax.shard_map(
        shards,
        mesh=mesh,
        in_specs=placed,
        out_specs=P("section", None, "expert", "tensor"),
        check_vma=False,
    )
```

```python
import jax
import jax.numpy as jnp
from jax import lax
from jax.sharding import PartitionSpec as P

D = 3072
EXPERTS = 8


def from_behind(block, axis, distance):
    devices = range(lax.axis_size(axis))
    route = [(i - distance, i) for i in devices if i - distance in devices]
    return lax.ppermute(block, axis, route)


def swap(block, axis, bit):
    n = lax.axis_size(axis)
    return lax.ppermute(block, axis, [(i, i ^ bit) for i in range(n)])


def shards(tokens, norm_gain, expert_ids, gate_weights, w_up, w_down):
    segments = lax.axis_size("section")
    n_exp = lax.axis_size("expert")
    segment_pos = lax.axis_index("section")
    t_pos = lax.axis_index("tensor")
    x_lo = t_pos // 2
    core = t_pos % 2
    micro = tokens.shape[0]
    rows_here = tokens.shape[1]
    quarter = tokens.shape[2]
    capacity = max(3 * rows_here // 8, 2 * rows_here // EXPERTS)
    up_local = w_up[0]
    down_local = w_down[0]
    local_count = up_local.shape[0]
    copies = n_exp * local_count // EXPERTS
    collected = jnp.zeros((micro, rows_here, quarter), jnp.bfloat16)
    total_steps = micro + segments - 1
    x_first = x_lo == 0
    core_first = core == 0

    def to_half(own, other):
        return jnp.where(
            x_first,
            jnp.concatenate([own, other], axis=-1),
            jnp.concatenate([other, own], axis=-1),
        )

    tokens_half = to_half(tokens, swap(tokens, "tensor", 2))
    gain_mine = to_half(norm_gain[0], swap(norm_gain[0], "tensor", 2))
    gain_theirs = swap(gain_mine, "tensor", 1)
    gain_first = jnp.where(core_first, gain_mine, gain_theirs)
    gain_second = jnp.where(core_first, gain_theirs, gain_mine)
    gain_full = jnp.concatenate(
        [gain_first[:quarter], gain_second[:quarter], gain_first[quarter:], gain_second[quarter:]]
    )
    routes_all = expert_ids[0].reshape(micro, -1)
    onehot_all = (routes_all[..., None] == jnp.arange(EXPERTS, dtype=jnp.int32)).astype(jnp.int32)
    slot_all = jnp.sum((jnp.cumsum(onehot_all, axis=1) - onehot_all) * onehot_all, axis=2)
    dest_all = routes_all * capacity + slot_all
    source_all = jnp.stack(
        [
            jnp.full((EXPERTS * capacity,), -1, jnp.int32)
            .at[dest_all[m]]
            .set(jnp.arange(2 * rows_here, dtype=jnp.int32) // 2)
            for m in range(micro)
        ]
    )
    n_t = lax.axis_size("tensor")
    cross_route = [
        (s * n_t + t, ((s + 1) % segments) * n_t + (t ^ 2)) for s in range(segments) for t in range(n_t)
    ]
    def layer_step(step, carried, collected):
        which = step - segment_pos
        which_safe = jnp.clip(which, 0, micro - 1)
        entering = lax.dynamic_index_in_dim(
            tokens_half, jnp.minimum(step, micro - 1), 0, keepdims=False
        )
        half_rows = jnp.where(segment_pos == 0, entering, carried)
        weights = lax.dynamic_index_in_dim(gate_weights[0], which_safe, 0, keepdims=False)
        dest = lax.dynamic_index_in_dim(dest_all, which_safe, 0, keepdims=False)
        source = lax.dynamic_index_in_dim(source_all, which_safe, 0, keepdims=False)
        filled = source >= 0
        outgoing = jnp.where(
            filled[:, None],
            jnp.take(half_rows, jnp.maximum(source, 0), axis=0),
            jnp.zeros((), jnp.bfloat16),
        )
        outgoing = outgoing.reshape(EXPERTS, capacity, 2 * quarter)
        outgoing = jnp.repeat(outgoing, copies, axis=0).reshape(
            n_exp, local_count, capacity, 2 * quarter
        )
        mine = lax.all_to_all(outgoing, "expert", split_axis=0, concat_axis=0, tiled=True)
        theirs = swap(mine, "tensor", 1)
        lo_q = lambda a: a[..., :quarter]
        hi_q = lambda a: a[..., quarter:]
        first = jnp.where(core_first, mine, theirs)
        second = jnp.where(core_first, theirs, mine)
        rows = jnp.concatenate([lo_q(first), lo_q(second), hi_q(first), hi_q(second)], axis=-1)
        rf = rows.astype(jnp.float32)
        sums = jnp.sum(rf * rf, axis=-1)
        normed = (rf * lax.rsqrt(sums / D + 1e-05)[..., None] * gain_full).astype(jnp.bfloat16)
        summed_up = jnp.einsum(
            "sekd,edf->sekf", normed, up_local, preferred_element_type=jnp.float32
        )
        hidden = jax.nn.silu(summed_up).astype(jnp.bfloat16)
        partial_out = jnp.einsum(
            "sekf,efd->sekd", hidden, down_local, preferred_element_type=jnp.float32
        )
        pq = [partial_out[..., q * quarter:(q + 1) * quarter] for q in range(4)]
        keep = jnp.where(
            core_first,
            jnp.concatenate([pq[0], pq[2]], axis=-1),
            jnp.concatenate([pq[1], pq[3]], axis=-1),
        )
        give = jnp.where(
            core_first,
            jnp.concatenate([pq[1], pq[3]], axis=-1),
            jnp.concatenate([pq[0], pq[2]], axis=-1),
        )
        got = swap(give.astype(jnp.bfloat16), "tensor", 1)
        chip_sum = (keep + got.astype(jnp.float32)).astype(jnp.bfloat16)
        returned = lax.all_to_all(chip_sum, "expert", split_axis=0, concat_axis=0, tiled=True)
        summed = jnp.sum(
            returned.reshape(EXPERTS, copies, capacity, 2 * quarter).astype(jnp.float32), axis=1
        )
        picked = jnp.take(summed.reshape(-1, 2 * quarter), dest, axis=0)
        picked = picked.reshape(rows_here, 2, 2 * quarter)
        y_half = jnp.sum(picked * weights[:, :, None], axis=1)
        y_keep = jnp.where(x_first, y_half[:, :quarter], y_half[:, quarter:])
        y_give = jnp.where(x_first, y_half[:, quarter:], y_half[:, :quarter])
        y_got = swap(y_give.astype(jnp.bfloat16), "tensor", 2).astype(jnp.float32)
        xf = jnp.where(x_first, half_rows[:, :quarter], half_rows[:, quarter:]).astype(jnp.float32)
        mixed = xf + (y_keep + y_got)
        produced = mixed.astype(jnp.bfloat16)
        chosen = (jnp.arange(micro, dtype=jnp.int32) == which)[:, None, None]
        collected = jnp.where(chosen, produced[None], collected)
        return produced, collected

    def looped(step, state):
        carried, collected = state
        produced, collected = layer_step(step, carried, collected)
        carried = to_half(
            lax.ppermute(produced, "section", [(i, (i + 1) % segments) for i in range(segments)]),
            lax.ppermute(produced, ("section", "tensor"), cross_route),
        )
        return carried, collected

    carried = jnp.zeros((rows_here, 2 * quarter), jnp.bfloat16)
    carried, collected = lax.fori_loop(0, total_steps - 1, looped, (carried, collected))
    _, collected = layer_step(total_steps - 1, carried, collected)
    return collected[None]


def solution(mesh):
    placed = (
        P(None, "expert", "tensor"),
        P("section", "tensor"),
        P("section", None, "expert", None),
        P("section", None, "expert", None),
        P("section", "expert", None, "tensor"),
        P("section", "expert", "tensor", None),
    )
    return jax.shard_map(
        shards,
        mesh=mesh,
        in_specs=placed,
        out_specs=P("section", None, "expert", "tensor"),
        check_vma=False,
    )
```

```python
import jax
import jax.numpy as jnp
from jax import lax
from jax.sharding import PartitionSpec as P

D = 3072
EXPERTS = 8


def from_behind(block, axis, distance):
    devices = range(lax.axis_size(axis))
    route = [(i - distance, i) for i in devices if i - distance in devices]
    return lax.ppermute(block, axis, route)


def swap(block, axis, bit):
    n = lax.axis_size(axis)
    return lax.ppermute(block, axis, [(i, i ^ bit) for i in range(n)])


def shards(tokens, norm_gain, expert_ids, gate_weights, w_up, w_down):
    segments = lax.axis_size("section")
    n_exp = lax.axis_size("expert")
    segment_pos = lax.axis_index("section")
    t_pos = lax.axis_index("tensor")
    x_lo = t_pos // 2
    core = t_pos % 2
    micro = tokens.shape[0]
    rows_here = tokens.shape[1]
    quarter = tokens.shape[2]
    capacity = max(3 * rows_here // 8, 2 * rows_here // EXPERTS)
    gain = norm_gain[0]
    gain_from = [gain, swap(gain, "tensor", 1), swap(gain, "tensor", 2), swap(gain, "tensor", 3)]
    gain_full = jnp.concatenate(
        [
            jnp.where(t_pos == q, gain_from[0],
                      jnp.where(t_pos ^ 1 == q, gain_from[1],
                                jnp.where(t_pos ^ 2 == q, gain_from[2], gain_from[3])))
            for q in range(4)
        ]
    )
    up_local = w_up[0]
    down_local = w_down[0]
    local_count = up_local.shape[0]
    copies = n_exp * local_count // EXPERTS
    collected = jnp.zeros((micro, rows_here, quarter), jnp.bfloat16)
    total_steps = micro + segments - 1
    x_first = x_lo == 0
    core_first = core == 0

    def to_half(own, other):
        return jnp.where(
            x_first,
            jnp.concatenate([own, other], axis=-1),
            jnp.concatenate([other, own], axis=-1),
        )

    tokens_half = to_half(tokens, swap(tokens, "tensor", 2))
    routes_all = expert_ids[0].reshape(micro, -1)
    onehot_all = (routes_all[..., None] == jnp.arange(EXPERTS, dtype=jnp.int32)).astype(jnp.int32)
    slot_all = jnp.sum((jnp.cumsum(onehot_all, axis=1) - onehot_all) * onehot_all, axis=2)
    dest_all = routes_all * capacity + slot_all
    source_all = jnp.stack(
        [
            jnp.full((EXPERTS * capacity,), -1, jnp.int32)
            .at[dest_all[m]]
            .set(jnp.arange(2 * rows_here, dtype=jnp.int32) // 2)
            for m in range(micro)
        ]
    )
    n_t = lax.axis_size("tensor")
    cross_route = [
        (s * n_t + t, ((s + 1) % segments) * n_t + (t ^ 2)) for s in range(segments) for t in range(n_t)
    ]
    def layer_step(step, carried, collected):
        which = step - segment_pos
        which_safe = jnp.clip(which, 0, micro - 1)
        entering = lax.dynamic_index_in_dim(
            tokens_half, jnp.minimum(step, micro - 1), 0, keepdims=False
        )
        half_rows = jnp.where(segment_pos == 0, entering, carried)
        weights = lax.dynamic_index_in_dim(gate_weights[0], which_safe, 0, keepdims=False)
        dest = lax.dynamic_index_in_dim(dest_all, which_safe, 0, keepdims=False)
        source = lax.dynamic_index_in_dim(source_all, which_safe, 0, keepdims=False)
        filled = source >= 0
        outgoing = jnp.where(
            filled[:, None],
            jnp.take(half_rows, jnp.maximum(source, 0), axis=0),
            jnp.zeros((), jnp.bfloat16),
        )
        outgoing = outgoing.reshape(EXPERTS, capacity, 2 * quarter)
        outgoing = jnp.repeat(outgoing, copies, axis=0).reshape(
            n_exp, local_count, capacity, 2 * quarter
        )
        mine = lax.all_to_all(outgoing, "expert", split_axis=0, concat_axis=0, tiled=True)
        theirs = swap(mine, "tensor", 1)
        lo_q = lambda a: a[..., :quarter]
        hi_q = lambda a: a[..., quarter:]
        first = jnp.where(core_first, mine, theirs)
        second = jnp.where(core_first, theirs, mine)
        rows = jnp.concatenate([lo_q(first), lo_q(second), hi_q(first), hi_q(second)], axis=-1)
        rf = rows.astype(jnp.float32)
        sums = jnp.sum(rf * rf, axis=-1)
        normed = (rf * lax.rsqrt(sums / D + 1e-05)[..., None] * gain_full).astype(jnp.bfloat16)
        summed_up = jnp.einsum(
            "sekd,edf->sekf", normed, up_local, preferred_element_type=jnp.float32
        )
        hidden = jax.nn.silu(summed_up).astype(jnp.bfloat16)
        partial_out = jnp.einsum(
            "sekf,efd->sekd", hidden, down_local, preferred_element_type=jnp.float32
        )
        pq = [partial_out[..., q * quarter:(q + 1) * quarter] for q in range(4)]
        keep = jnp.where(
            core_first,
            jnp.concatenate([pq[0], pq[2]], axis=-1),
            jnp.concatenate([pq[1], pq[3]], axis=-1),
        )
        give = jnp.where(
            core_first,
            jnp.concatenate([pq[1], pq[3]], axis=-1),
            jnp.concatenate([pq[0], pq[2]], axis=-1),
        )
        got = swap(give.astype(jnp.bfloat16), "tensor", 1)
        chip_sum = (keep + got.astype(jnp.float32)).astype(jnp.bfloat16)
        returned = lax.all_to_all(chip_sum, "expert", split_axis=0, concat_axis=0, tiled=True)
        summed = jnp.sum(
            returned.reshape(EXPERTS, copies, capacity, 2 * quarter).astype(jnp.float32), axis=1
        )
        picked = jnp.take(summed.reshape(-1, 2 * quarter), dest, axis=0)
        picked = picked.reshape(rows_here, 2, 2 * quarter)
        y_half = jnp.sum(picked * weights[:, :, None], axis=1)
        y_keep = jnp.where(x_first, y_half[:, :quarter], y_half[:, quarter:])
        y_give = jnp.where(x_first, y_half[:, quarter:], y_half[:, :quarter])
        y_got = swap(y_give.astype(jnp.bfloat16), "tensor", 2).astype(jnp.float32)
        xf = jnp.where(x_first, half_rows[:, :quarter], half_rows[:, quarter:]).astype(jnp.float32)
        mixed = xf + (y_keep + y_got)
        produced = mixed.astype(jnp.bfloat16)
        chosen = (jnp.arange(micro, dtype=jnp.int32) == which)[:, None, None]
        collected = jnp.where(chosen, produced[None], collected)
        return produced, collected

    def looped(step, state):
        carried, collected = state
        produced, collected = layer_step(step, carried, collected)
        carried = to_half(
            lax.ppermute(produced, "section", [(i, (i + 1) % segments) for i in range(segments)]),
            lax.ppermute(produced, ("section", "tensor"), cross_route),
        )
        return carried, collected

    carried = jnp.zeros((rows_here, 2 * quarter), jnp.bfloat16)
    for step in range(total_steps - 1):
        carried, collected = looped(step, (carried, collected))
    _, collected = layer_step(total_steps - 1, carried, collected)
    return collected[None]


def solution(mesh):
    placed = (
        P(None, "expert", "tensor"),
        P("section", "tensor"),
        P("section", None, "expert", None),
        P("section", None, "expert", None),
        P("section", "expert", None, "tensor"),
        P("section", "expert", "tensor", None),
    )
    return jax.shard_map(
        shards,
        mesh=mesh,
        in_specs=placed,
        out_specs=P("section", None, "expert", "tensor"),
        check_vma=False,
    )
```
